32 devices in a mesh: uv: 8 (over y, x, core), chan: 4 (over z).
Axes of the slice: x: 2, y: 2, z: 4, core: 2. Of those that a mesh axis runs over, the one named last changes fastest.
Arguments:
- vis: bfloat16 [98304, 2, 1024], P('uv', None, 'chan'), may hold values from -6 to 6
- row_cell: int32 [98304], P('uv'), may hold values from 0 to 127
- tap_weight: bfloat16 [8, 98304], P(None, 'uv'), may hold values from 0.029907227 to 0.29882812
- tap_offset: int32 [8], replicated, may hold values from -32 to 32
- block_tile: int32 [768], P('uv'), may hold values from 0 to 79, as said below
- tile_owner: int32 [80], replicated, may hold values from 0 to 7, as said below
- galaxy: bfloat16 [152, 128, 2048], P('uv', 'chan'), may hold values from -6 to 6
Outputs:
- delay_cube: bfloat16 [152, 128, 2048], P('uv', 'chan')
- cross_power: float32 [152, 1024], P('uv')
The draws below stay inside these ranges and needn't reach their ends.
Inputs may be any that keep to these rules, and one draw needn't show every extreme that they name: `tile_owner`: each of the 8 owners holds 1 to 19 tiles, and some owner exactly 19. `block_tile`: of the 96 row blocks of one index of uv, at most 22 lie in tiles of one owner, and exactly 22 lie in the tiles of some owner.
All inputs are finite; a program needn't handle non-finite values.
Results may differ from the reference program's by a relative error of at most 0.0059.
Values may be sent and summed in bfloat16 or wider, within the bound.
No kernel may reach another device: no remote copies, remote signals or barrier semaphores. Data moves between devices by JAX's collectives and lax.ppermute only.
A program may use at most 128 MiB of HBM per device.

```python
import math
import jax
import jax.numpy as jnp
from jax import lax

CH = 1024
BR = 128
TC = 128
KT = 8
NB_DEV = 96
TILES_DEV = 10
ROWS = 98304
NTILES = 80
MAXT = 19
SLOTS = 152
N_UV = 8


def ownership(key):
    base = jax.random.fold_in(key, 7)
    key_perm, key_delta, key_shuffle = jax.random.split(base, 3)
    half = N_UV // 2
    mean_load = NB_DEV // N_UV
    owners = jax.random.permutation(key_perm, N_UV).astype(jnp.int32)
    delta = jax.random.randint(key_delta, (half,), 0, TILES_DEV).astype(jnp.int32)
    delta = delta.at[0].set(TILES_DEV - 1)
    extra = delta * mean_load // TILES_DEV
    counts_perm = jnp.concatenate([TILES_DEV + delta, TILES_DEV - delta])
    quota_perm = jnp.concatenate([mean_load + extra, mean_load - extra])
    counts = jnp.zeros((N_UV,), jnp.int32).at[owners].set(counts_perm)
    quota = jnp.zeros((N_UV,), jnp.int32).at[owners].set(quota_perm)
    owner_seq = jnp.repeat(jnp.arange(N_UV, dtype=jnp.int32), counts, total_repeat_length=NTILES)
    tile_owner = jax.random.permutation(key_shuffle, owner_seq).astype(jnp.int32)
    return (tile_owner, counts, quota)


def draw_tile_owner(key, part):
    return ownership(key)[0]


def draw_block_tile(key, part):
    tile_owner, counts, quota = ownership(key)
    by_owner = jnp.argsort(tile_owner, stable=True).astype(jnp.int32)
    start = (jnp.cumsum(counts) - counts).astype(jnp.int32)

    def one_source(source_key):
        key_order, key_pick = jax.random.split(source_key)
        seq = jnp.repeat(jnp.arange(N_UV, dtype=jnp.int32), quota, total_repeat_length=NB_DEV)
        seq = jax.random.permutation(key_order, seq)
        pick = jax.random.randint(key_pick, (NB_DEV,), 0, counts[seq]).astype(jnp.int32)
        return by_owner[start[seq] + pick]
    keys = jax.random.split(jax.random.fold_in(key, 11), N_UV)
    return jax.vmap(one_source)(keys).reshape(-1).astype(jnp.int32)


def draw_vis(key, part):
    key_vals = jax.random.fold_in(jax.random.fold_in(key, 3), 0)
    channel = jnp.arange(CH, dtype=jnp.int32)
    edge = CH // 8
    inner = (channel >= edge) & (channel < CH - edge)
    factor = jnp.where(inner, jnp.float32(0.05), jnp.float32(1.0)).astype(jnp.float32)
    values = jnp.clip(jax.random.normal(key_vals, (ROWS, 2, CH), jnp.float32), -6.0, 6.0)
    return (values * factor[None, None, :]).astype(jnp.bfloat16)


def set_ends(array, rng, low, largest):
    shape = array.shape
    index_at = [jax.random.randint(jax.random.fold_in(rng, axis), (), 0, shape[axis]) for axis in range(len(shape))]
    array = array.at[tuple(index_at)].set(low)
    longest = shape.index(max(shape))
    index_at[longest] = (index_at[longest] + 1) % shape[longest]
    return array.at[tuple(index_at)].set(largest)


def block_scale(own_key, shape, cuts, least, largest):
    level = 1.0
    for dim, blocks in cuts:
        draws = jax.random.uniform(jax.random.fold_in(jax.random.fold_in(own_key, 6), dim), (blocks,), jnp.float32, least / len(cuts), largest / len(cuts))
        level = level * jnp.repeat(jnp.exp(draws), shape[dim] // blocks).reshape((-1,) + (1,) * (len(shape) - 1 - dim))
    return level


def normal_values(stream_key, dims, spread, reach, pieces=(), held_as=jnp.bfloat16):
    factor_of = block_scale(stream_key, dims, pieces, -0.22, 0.18) if pieces else 1.0
    values = jax.random.normal(stream_key, dims, jnp.float32) * spread * factor_of
    return jnp.minimum(jnp.maximum(values, -reach), reach).astype(held_as)


def setup_inputs(seed: int = 0) -> dict:
    key_of = jax.random.split(jax.random.key(seed), 8)
    return {
        "vis": draw_vis(jax.random.fold_in(key_of[7], 71), 0),
        "row_cell": set_ends(jax.random.randint(key_of[1], (ROWS,), 0, TC), jax.random.fold_in(key_of[1], 1), 0, TC - 1).astype(jnp.int32),
        "tap_weight": jnp.clip(jnp.exp(math.log(0.29882812) - 2.30176843 * jax.random.uniform(key_of[2], (KT, ROWS), jnp.float32) ** block_scale(key_of[2], (KT, ROWS), ((1, 8),), -0.2, 0.2)), 0.029907227, 0.29882812).astype(jnp.bfloat16),
        "tap_offset": set_ends(jax.random.randint(key_of[3], (KT,), -(TC // 4), TC // 4 + 1), jax.random.fold_in(key_of[3], 1), -(TC // 4), (TC // 4 + 1) - 1).astype(jnp.int32),
        "block_tile": draw_block_tile(jax.random.fold_in(key_of[7], 71), 0),
        "tile_owner": draw_tile_owner(jax.random.fold_in(key_of[7], 71), 0),
        "galaxy": normal_values(key_of[6], (SLOTS, TC, 2 * CH), 1.0, 6.0, ((0, 8), (1, 4))),
    }


def tile_ranks(tile_owner, owners):
    onehot = (tile_owner[:, None] == jnp.arange(owners, dtype=jnp.int32)[None, :]).astype(jnp.int32)
    before = jnp.cumsum(onehot, axis=0) - onehot
    return lax.optimization_barrier(jnp.sum(before * onehot, axis=1)).astype(jnp.int32)

def kernel_matrix(cells, weights, tap_offset):
    positions = jnp.arange(TC, dtype=jnp.int32)
    total = jnp.zeros(cells.shape[:-1] + (TC, cells.shape[-1]), jnp.float32)
    for k in range(KT):
        target = cells + tap_offset[k]
        hit = target[..., None, :] == positions[:, None]
        total = total + jnp.where(hit, weights[..., k, :].astype(jnp.float32)[..., None, :], jnp.float32(0.0))
    return total.astype(jnp.bfloat16)

def delay_table():
    freq = jnp.arange(CH, dtype=jnp.int32)
    phase = (freq[:, None] * freq[None, :] % CH).astype(jnp.float32) * jnp.float32(2.0 * math.pi / CH)
    cosine = jnp.cos(phase)
    sine = jnp.sin(phase)
    x = freq.astype(jnp.float32) * jnp.float32(2.0 * math.pi / CH)
    taper = 0.35875 - 0.48829 * jnp.cos(x) + 0.14128 * jnp.cos(2.0 * x) - 0.01168 * jnp.cos(3.0 * x)
    scale = (taper / jnp.float32(math.sqrt(CH)))[:, None]
    upper = jnp.concatenate([cosine * scale, -sine * scale], axis=1)
    lower = jnp.concatenate([sine * scale, cosine * scale], axis=1)
    return jnp.concatenate([upper, lower], axis=0).astype(jnp.bfloat16)

def reference(vis, row_cell, tap_weight, tap_offset, block_tile, tile_owner, galaxy):
    nblocks = block_tile.shape[0]
    vis_blocks = vis.reshape(nblocks, BR, 2 * CH)
    cells = row_cell.reshape(nblocks, BR)
    weights = jnp.transpose(tap_weight.reshape(KT, nblocks, BR), (1, 0, 2))

    def grid_step(grid, item):
        block_vis, block_cells, block_weights, tile = item
        matrix = kernel_matrix(block_cells, block_weights, tap_offset)
        term = jnp.dot(matrix, block_vis, preferred_element_type=jnp.float32)
        return (grid.at[tile].add(term), None)
    grid, _ = lax.scan(grid_step, jnp.zeros((NTILES, TC, 2 * CH), jnp.float32), (vis_blocks, cells, weights, block_tile))
    gridded = grid.astype(jnp.bfloat16)
    delay = jnp.dot(gridded.reshape(NTILES * TC, 2 * CH), delay_table(), preferred_element_type=jnp.float32).reshape(NTILES, TC, 2 * CH)
    slots = (tile_owner * MAXT + tile_ranks(tile_owner, N_UV)).astype(jnp.int32)
    gal = galaxy[slots].astype(jnp.float32)
    product = delay[..., :CH] * gal[..., :CH] + delay[..., CH:] * gal[..., CH:]
    power_tiles = lax.optimization_barrier(jnp.sum(product, axis=1)) / jnp.float32(math.sqrt(TC))
    cube = jnp.zeros((SLOTS, TC, 2 * CH), jnp.bfloat16).at[slots].set(delay.astype(jnp.bfloat16))
    power = jnp.zeros((SLOTS, CH), jnp.float32).at[slots].set(power_tiles)
    return (cube, power)
```

```python
import math

import jax
import jax.numpy as jnp
from jax import lax
from jax.sharding import PartitionSpec as P

CH = 1024
BR = 128
TC = 128
KT = 8


def tile_ranks(tile_owner, owners):
    onehot = (tile_owner[:, None] == jnp.arange(owners, dtype=jnp.int32)[None, :]).astype(jnp.int32)
    before = jnp.cumsum(onehot, axis=0) - onehot
    return jnp.sum(before * onehot, axis=1)


def kernel_matrix(cells, weights, tap_offset):
    positions = jnp.arange(TC, dtype=jnp.int32)
    total = jnp.zeros(cells.shape[:-1] + (TC, cells.shape[-1]), jnp.float32)
    for k in range(KT):
        target = cells + tap_offset[k]
        hit = target[..., None, :] == positions[:, None]
        total = total + jnp.where(
            hit, weights[..., k, :].astype(jnp.float32)[..., None, :], jnp.float32(0.0)
        )
    return total.astype(jnp.bfloat16)


def delay_table():
    freq = jnp.arange(CH, dtype=jnp.int32)
    phase = (freq[:, None] * freq[None, :] % CH).astype(jnp.float32) * jnp.float32(
        2.0 * math.pi / CH
    )
    cosine = jnp.cos(phase)
    sine = jnp.sin(phase)
    x = freq.astype(jnp.float32) * jnp.float32(2.0 * math.pi / CH)
    taper = 0.35875 - 0.48829 * jnp.cos(x) + 0.14128 * jnp.cos(2.0 * x) - 0.01168 * jnp.cos(3.0 * x)
    scale = (taper / jnp.float32(math.sqrt(CH)))[:, None]
    upper = jnp.concatenate([cosine * scale, -sine * scale], axis=1)
    lower = jnp.concatenate([sine * scale, cosine * scale], axis=1)
    return jnp.concatenate([upper, lower], axis=0).astype(jnp.bfloat16)


def _partner_pairs(n, fn):
    return [(i, fn(i)) for i in range(n)]


def _allreduce_sum(x, axis, n):
    if n & (n - 1):
        return lax.psum(x, axis)
    d = 1
    while d < n:
        x = x + lax.ppermute(x, axis, _partner_pairs(n, lambda i, d=d: i ^ d))
        d *= 2
    return x


def body(vis, row_cell, tap_weight, tap_offset, block_tile, tile_owner, galaxy):
    n_owners = lax.axis_size("uv")
    n_chan = lax.axis_size("chan")
    pairs = n_owners // 2
    me = lax.axis_index("uv")
    parity = me % 2
    chip = me // 2
    nblocks = block_tile.shape[0]
    slots_dev = galaxy.shape[0]
    chan_dev = vis.shape[2]
    width = 2 * chan_dev

    rank_of_tile = tile_ranks(tile_owner, n_owners)
    owner = tile_owner[block_tile]
    rank = rank_of_tile[block_tile]
    slot = (owner % 2) * (pairs * slots_dev) + (owner // 2) * slots_dev + rank
    n_slots = n_owners * slots_dev
    pick = (jnp.arange(n_slots, dtype=jnp.int32)[:, None] == slot[None, :]).astype(jnp.bfloat16)

    blocks = vis.reshape(nblocks, BR, width)
    cells = row_cell.reshape(nblocks, BR)
    weights = jnp.transpose(tap_weight.reshape(KT, nblocks, BR), (1, 0, 2))
    matrix = kernel_matrix(cells, weights, tap_offset)
    contrib = jnp.einsum("bcr,brf->bcf", matrix, blocks, preferred_element_type=jnp.float32)
    contrib = contrib.reshape(nblocks, TC * width)
    high = contrib.astype(jnp.bfloat16)
    low = (contrib - high.astype(jnp.float32)).astype(jnp.bfloat16)
    partial = jnp.dot(
        jnp.concatenate([pick, pick], axis=1),
        jnp.concatenate([high, low], axis=0),
        preferred_element_type=jnp.float32,
    ).astype(jnp.bfloat16)
    partial = partial.reshape(2, pairs, slots_dev, TC, width)

    mine = lax.dynamic_index_in_dim(partial, parity, axis=0, keepdims=False)
    other = lax.dynamic_index_in_dim(partial, 1 - parity, axis=0, keepdims=False)
    got = lax.ppermute(other, "uv", _partner_pairs(n_owners, lambda i: i ^ 1))
    pair_sum = mine.astype(jnp.float32) + got.astype(jnp.float32)
    pair_send = pair_sum.astype(jnp.bfloat16)

    grid = lax.dynamic_index_in_dim(pair_sum, chip, axis=0, keepdims=False)
    for d in range(1, pairs):
        if pairs & (pairs - 1):
            dest = lambda c, d=d: (c + d) % pairs
            src_chip = (chip - d) % pairs
        else:
            dest = lambda c, d=d: c ^ d
            src_chip = chip ^ d
        del src_chip
        send = lax.dynamic_index_in_dim(pair_send, dest(chip), axis=0, keepdims=False)
        recv = lax.ppermute(
            send, "uv", _partner_pairs(n_owners, lambda i, dest=dest: dest(i // 2) * 2 + i % 2)
        )
        grid = grid + recv.astype(jnp.float32)

    gridded = grid.astype(jnp.bfloat16).reshape(slots_dev, TC, 2, chan_dev)
    table = delay_table()
    piece = lax.all_to_all(gridded, "chan", split_axis=1, concat_axis=3, tiled=True)
    count = piece.shape[0]
    cells_part = piece.shape[1]
    flat = piece.reshape(count * cells_part, 2 * CH)
    out = jnp.dot(flat, table, preferred_element_type=jnp.float32)
    delay = out.reshape(count, cells_part, 2 * CH)
    galaxy_f = galaxy.astype(jnp.float32)
    product = delay[..., :CH] * galaxy_f[..., :CH] + delay[..., CH:] * galaxy_f[..., CH:]
    local_power = jnp.sum(product, axis=1)
    power = _allreduce_sum(local_power, "chan", n_chan) / jnp.float32(math.sqrt(TC))
    return (delay.astype(jnp.bfloat16), power)


def solution(mesh):
    return jax.shard_map(
        body,
        mesh=mesh,
        in_specs=(
            P("uv", None, "chan"),
            P("uv"),
            P(None, "uv"),
            P(),
            P("uv"),
            P(),
            P("uv", "chan", None),
        ),
        out_specs=(P("uv", "chan", None), P("uv", None)),
        check_vma=False,
    )
```

```python
import math

import jax
import jax.numpy as jnp
from jax import lax
from jax.sharding import PartitionSpec as P

CH = 1024
BR = 128
TC = 128
KT = 8


def tile_ranks(tile_owner, owners):
    onehot = (tile_owner[:, None] == jnp.arange(owners, dtype=jnp.int32)[None, :]).astype(jnp.int32)
    before = jnp.cumsum(onehot, axis=0) - onehot
    return jnp.sum(before * onehot, axis=1)


def kernel_matrix(cells, weights, tap_offset):
    positions = jnp.arange(TC, dtype=jnp.int32)
    total = jnp.zeros(cells.shape[:-1] + (TC, cells.shape[-1]), jnp.float32)
    for k in range(KT):
        target = cells + tap_offset[k]
        hit = target[..., None, :] == positions[:, None]
        total = total + jnp.where(
            hit, weights[..., k, :].astype(jnp.float32)[..., None, :], jnp.float32(0.0)
        )
    return total.astype(jnp.bfloat16)


def delay_table():
    freq = jnp.arange(CH, dtype=jnp.int32)
    phase = (freq[:, None] * freq[None, :] % CH).astype(jnp.float32) * jnp.float32(
        2.0 * math.pi / CH
    )
    cosine = jnp.cos(phase)
    sine = jnp.sin(phase)
    x = freq.astype(jnp.float32) * jnp.float32(2.0 * math.pi / CH)
    taper = 0.35875 - 0.48829 * jnp.cos(x) + 0.14128 * jnp.cos(2.0 * x) - 0.01168 * jnp.cos(3.0 * x)
    scale = (taper / jnp.float32(math.sqrt(CH)))[:, None]
    upper = jnp.concatenate([cosine * scale, -sine * scale], axis=1)
    lower = jnp.concatenate([sine * scale, cosine * scale], axis=1)
    return jnp.concatenate([upper, lower], axis=0).astype(jnp.bfloat16)


def _partner_pairs(n, fn):
    return [(i, fn(i)) for i in range(n)]


def _allreduce_sum(x, axis, n):
    if n & (n - 1):
        return lax.psum(x, axis)
    d = 1
    while d < n:
        x = x + lax.ppermute(x, axis, _partner_pairs(n, lambda i, d=d: i ^ d))
        d *= 2
    return x


def _chunk(part, matrix, pick2, parity, chip, n_owners, slots_dev):
    pairs = n_owners // 2
    contrib = jnp.einsum("bcr,brf->bcf", matrix, part, preferred_element_type=jnp.float32)
    high = contrib.astype(jnp.bfloat16)
    low = (contrib - high.astype(jnp.float32)).astype(jnp.bfloat16)
    partial = jnp.einsum(
        "sb,bcf->scf",
        pick2,
        jnp.concatenate([high, low], axis=0),
        preferred_element_type=jnp.float32,
    ).astype(jnp.bfloat16)
    partial = partial.reshape((2, pairs, slots_dev) + partial.shape[1:])

    mine = lax.dynamic_index_in_dim(partial, parity, axis=0, keepdims=False)
    other = lax.dynamic_index_in_dim(partial, 1 - parity, axis=0, keepdims=False)
    got = lax.ppermute(other, "uv", _partner_pairs(n_owners, lambda i: i ^ 1))
    pair_sum = mine.astype(jnp.float32) + got.astype(jnp.float32)
    pair_send = pair_sum.astype(jnp.bfloat16)

    grid = lax.dynamic_index_in_dim(pair_sum, chip, axis=0, keepdims=False)
    for d in range(1, pairs):
        if pairs & (pairs - 1):
            dest = lambda c, d=d: (c + d) % pairs
        else:
            dest = lambda c, d=d: c ^ d
        send = lax.dynamic_index_in_dim(pair_send, dest(chip), axis=0, keepdims=False)
        recv = lax.ppermute(
            send, "uv", _partner_pairs(n_owners, lambda i, dest=dest: dest(i // 2) * 2 + i % 2)
        )
        grid = grid + recv.astype(jnp.float32)
    gridded = grid.astype(jnp.bfloat16)
    return lax.all_to_all(gridded, "chan", split_axis=1, concat_axis=2, tiled=True)


def body(vis, row_cell, tap_weight, tap_offset, block_tile, tile_owner, galaxy):
    n_owners = lax.axis_size("uv")
    n_chan = lax.axis_size("chan")
    pairs = n_owners // 2
    me = lax.axis_index("uv")
    parity = me % 2
    chip = me // 2
    nblocks = block_tile.shape[0]
    slots_dev = galaxy.shape[0]
    chan_dev = vis.shape[2]

    rank_of_tile = tile_ranks(tile_owner, n_owners)
    owner = tile_owner[block_tile]
    rank = rank_of_tile[block_tile]
    slot = (owner % 2) * (pairs * slots_dev) + (owner // 2) * slots_dev + rank
    n_slots = n_owners * slots_dev
    pick = (jnp.arange(n_slots, dtype=jnp.int32)[:, None] == slot[None, :]).astype(jnp.bfloat16)
    pick2 = jnp.concatenate([pick, pick], axis=1)

    blocks = vis.reshape(nblocks, BR, 2, chan_dev)
    cells = row_cell.reshape(nblocks, BR)
    weights = jnp.transpose(tap_weight.reshape(KT, nblocks, BR), (1, 0, 2))
    matrix = kernel_matrix(cells, weights, tap_offset)
    table = delay_table()
    out = None
    for k in range(2):
        piece = _chunk(blocks[:, :, k, :], matrix, pick2, parity, chip, n_owners, slots_dev)
        count, cells_part = piece.shape[0], piece.shape[1]
        term = jnp.dot(
            piece.reshape(count * cells_part, CH),
            table[k * CH:(k + 1) * CH],
            preferred_element_type=jnp.float32,
        )
        out = term if out is None else out + term
    delay = out.reshape(count, cells_part, 2 * CH)
    galaxy_f = galaxy.astype(jnp.float32)
    product = delay[..., :CH] * galaxy_f[..., :CH] + delay[..., CH:] * galaxy_f[..., CH:]
    local_power = jnp.sum(product, axis=1)
    power = _allreduce_sum(local_power, "chan", n_chan) / jnp.float32(math.sqrt(TC))
    return (delay.astype(jnp.bfloat16), power)


def solution(mesh):
    return jax.shard_map(
        body,
        mesh=mesh,
        in_specs=(
            P("uv", None, "chan"),
            P("uv"),
            P(None, "uv"),
            P(),
            P("uv"),
            P(),
            P("uv", "chan", None),
        ),
        out_specs=(P("uv", "chan", None), P("uv", None)),
        check_vma=False,
    )
```

```python
import math

import jax
import jax.numpy as jnp
from jax import lax
from jax.sharding import PartitionSpec as P

CH = 1024
BR = 128
TC = 128
KT = 8


def tile_ranks(tile_owner, owners):
    onehot = (tile_owner[:, None] == jnp.arange(owners, dtype=jnp.int32)[None, :]).astype(jnp.int32)
    before = jnp.cumsum(onehot, axis=0) - onehot
    return jnp.sum(before * onehot, axis=1)


def kernel_matrix(cells, weights, tap_offset):
    positions = jnp.arange(TC, dtype=jnp.int32)
    total = jnp.zeros(cells.shape[:-1] + (TC, cells.shape[-1]), jnp.float32)
    for k in range(KT):
        target = cells + tap_offset[k]
        hit = target[..., None, :] == positions[:, None]
        total = total + jnp.where(
            hit, weights[..., k, :].astype(jnp.float32)[..., None, :], jnp.float32(0.0)
        )
    return total.astype(jnp.bfloat16)


def delay_table():
    freq = jnp.arange(CH, dtype=jnp.int32)
    phase = (freq[:, None] * freq[None, :] % CH).astype(jnp.float32) * jnp.float32(
        2.0 * math.pi / CH
    )
    cosine = jnp.cos(phase)
    sine = jnp.sin(phase)
    x = freq.astype(jnp.float32) * jnp.float32(2.0 * math.pi / CH)
    taper = 0.35875 - 0.48829 * jnp.cos(x) + 0.14128 * jnp.cos(2.0 * x) - 0.01168 * jnp.cos(3.0 * x)
    scale = (taper / jnp.float32(math.sqrt(CH)))[:, None]
    upper = jnp.concatenate([cosine * scale, -sine * scale], axis=1)
    lower = jnp.concatenate([sine * scale, cosine * scale], axis=1)
    return jnp.concatenate([upper, lower], axis=0).astype(jnp.bfloat16)


def _partner_pairs(n, fn):
    return [(i, fn(i)) for i in range(n)]


def _allreduce_sum(x, axis, n):
    if n & (n - 1):
        return lax.psum(x, axis)
    d = 1
    while d < n:
        x = x + lax.ppermute(x, axis, _partner_pairs(n, lambda i, d=d: i ^ d))
        d *= 2
    return x


def _gather_pair(part, matrix, pick2, parity, chip, n_owners, slots_dev):
    pairs = n_owners // 2
    contrib = jnp.einsum("bcr,brf->bcf", matrix, part, preferred_element_type=jnp.float32)
    high = contrib.astype(jnp.bfloat16)
    low = (contrib - high.astype(jnp.float32)).astype(jnp.bfloat16)
    partial = jnp.einsum(
        "sb,bcf->scf",
        pick2,
        jnp.concatenate([high, low], axis=0),
        preferred_element_type=jnp.float32,
    ).astype(jnp.bfloat16)
    partial = partial.reshape((2, pairs, slots_dev) + partial.shape[1:])

    mine = lax.dynamic_index_in_dim(partial, parity, axis=0, keepdims=False)
    other = lax.dynamic_index_in_dim(partial, 1 - parity, axis=0, keepdims=False)
    got = lax.ppermute(other, "uv", _partner_pairs(n_owners, lambda i: i ^ 1))
    pair_send = (mine.astype(jnp.float32) + got.astype(jnp.float32)).astype(jnp.bfloat16)
    own = lax.dynamic_index_in_dim(mine, chip, axis=0, keepdims=False).astype(
        jnp.float32
    ) + lax.dynamic_index_in_dim(got, chip, axis=0, keepdims=False).astype(jnp.float32)
    return pair_send, own


def _scatter_pairs(pair_send, own, chip, n_owners):
    pairs = n_owners // 2
    grid = own
    for d in range(1, pairs):
        if pairs & (pairs - 1):
            dest = lambda c, d=d: (c + d) % pairs
        else:
            dest = lambda c, d=d: c ^ d
        send = lax.dynamic_index_in_dim(pair_send, dest(chip), axis=0, keepdims=False)
        recv = lax.ppermute(
            send, "uv", _partner_pairs(n_owners, lambda i, dest=dest: dest(i // 2) * 2 + i % 2)
        )
        grid = grid + recv.astype(jnp.float32)
    gridded = grid.astype(jnp.bfloat16)
    return lax.all_to_all(gridded, "chan", split_axis=1, concat_axis=2, tiled=True)


def body(vis, row_cell, tap_weight, tap_offset, block_tile, tile_owner, galaxy):
    n_owners = lax.axis_size("uv")
    n_chan = lax.axis_size("chan")
    pairs = n_owners // 2
    me = lax.axis_index("uv")
    parity = me % 2
    chip = me // 2
    nblocks = block_tile.shape[0]
    slots_dev = galaxy.shape[0]
    chan_dev = vis.shape[2]

    rank_of_tile = tile_ranks(tile_owner, n_owners)
    owner = tile_owner[block_tile]
    rank = rank_of_tile[block_tile]
    slot = (owner % 2) * (pairs * slots_dev) + (owner // 2) * slots_dev + rank
    n_slots = n_owners * slots_dev
    pick = (jnp.arange(n_slots, dtype=jnp.int32)[:, None] == slot[None, :]).astype(jnp.bfloat16)
    pick2 = jnp.concatenate([pick, pick], axis=1)

    blocks = vis.reshape(nblocks, BR, 2, chan_dev)
    cells = row_cell.reshape(nblocks, BR)
    weights = jnp.transpose(tap_weight.reshape(KT, nblocks, BR), (1, 0, 2))
    matrix = kernel_matrix(cells, weights, tap_offset)
    table = delay_table()
    first = _gather_pair(blocks[:, :, 0, :], matrix, pick2, parity, chip, n_owners, slots_dev)
    second = _gather_pair(blocks[:, :, 1, :], matrix, pick2, parity, chip, n_owners, slots_dev)
    out = None
    for k, (pair_send, own) in enumerate((first, second)):
        piece = _scatter_pairs(pair_send, own, chip, n_owners)
        count, cells_part = piece.shape[0], piece.shape[1]
        term = jnp.dot(
            piece.reshape(count * cells_part, CH),
            table[k * CH:(k + 1) * CH],
            preferred_element_type=jnp.float32,
        )
        out = term if out is None else out + term
    delay = out.reshape(count, cells_part, 2 * CH)
    galaxy_f = galaxy.astype(jnp.float32)
    product = delay[..., :CH] * galaxy_f[..., :CH] + delay[..., CH:] * galaxy_f[..., CH:]
    local_power = jnp.sum(product, axis=1)
    power = _allreduce_sum(local_power, "chan", n_chan) / jnp.float32(math.sqrt(TC))
    return (delay.astype(jnp.bfloat16), power)


def solution(mesh):
    return jax.shard_map(
        body,
        mesh=mesh,
        in_specs=(
            P("uv", None, "chan"),
            P("uv"),
            P(None, "uv"),
            P(),
            P("uv"),
            P(),
            P("uv", "chan", None),
        ),
        out_specs=(P("uv", "chan", None), P("uv", None)),
        check_vma=False,
    )
```

```python
import math

import jax
import jax.numpy as jnp
from jax import lax
from jax.sharding import PartitionSpec as P

CH = 1024
BR = 128
TC = 128
KT = 8


def tile_ranks(tile_owner, owners):
    onehot = (tile_owner[:, None] == jnp.arange(owners, dtype=jnp.int32)[None, :]).astype(jnp.int32)
    before = jnp.cumsum(onehot, axis=0) - onehot
    return jnp.sum(before * onehot, axis=1)


def kernel_matrix(cells, weights, tap_offset):
    positions = jnp.arange(TC, dtype=jnp.int32)
    total = jnp.zeros(cells.shape[:-1] + (TC, cells.shape[-1]), jnp.float32)
    for k in range(KT):
        target = cells + tap_offset[k]
        hit = target[..., None, :] == positions[:, None]
        total = total + jnp.where(
            hit, weights[..., k, :].astype(jnp.float32)[..., None, :], jnp.float32(0.0)
        )
    return total.astype(jnp.bfloat16)


def delay_table():
    freq = jnp.arange(CH, dtype=jnp.int32)
    phase = (freq[:, None] * freq[None, :] % CH).astype(jnp.float32) * jnp.float32(
        2.0 * math.pi / CH
    )
    cosine = jnp.cos(phase)
    sine = jnp.sin(phase)
    x = freq.astype(jnp.float32) * jnp.float32(2.0 * math.pi / CH)
    taper = 0.35875 - 0.48829 * jnp.cos(x) + 0.14128 * jnp.cos(2.0 * x) - 0.01168 * jnp.cos(3.0 * x)
    scale = (taper / jnp.float32(math.sqrt(CH)))[:, None]
    upper = jnp.concatenate([cosine * scale, -sine * scale], axis=1)
    lower = jnp.concatenate([sine * scale, cosine * scale], axis=1)
    return jnp.concatenate([upper, lower], axis=0).astype(jnp.bfloat16)


def _partner_pairs(n, fn):
    return [(i, fn(i)) for i in range(n)]


def _allreduce_sum(x, axis, n):
    if n & (n - 1):
        return lax.psum(x, axis)
    d = 1
    while d < n:
        x = x + lax.ppermute(x, axis, _partner_pairs(n, lambda i, d=d: i ^ d))
        d *= 2
    return x


def _gather_pair(part, matrix, pick2, parity, chip, n_owners, slots_dev):
    pairs = n_owners // 2
    contrib = jnp.einsum("bcr,brf->bcf", matrix, part, preferred_element_type=jnp.float32)
    high = contrib.astype(jnp.bfloat16)
    low = (contrib - high.astype(jnp.float32)).astype(jnp.bfloat16)
    partial = jnp.einsum(
        "sb,bcf->scf",
        pick2,
        jnp.concatenate([high, low], axis=0),
        preferred_element_type=jnp.float32,
    ).astype(jnp.bfloat16)
    partial = partial.reshape((2, pairs, slots_dev) + partial.shape[1:])

    mine = lax.dynamic_index_in_dim(partial, parity, axis=0, keepdims=False)
    other = lax.dynamic_index_in_dim(partial, 1 - parity, axis=0, keepdims=False)
    got = lax.ppermute(other, "uv", _partner_pairs(n_owners, lambda i: i ^ 1))
    return mine, got


def _halving(mine, got, chip, n_owners, order):
    pairs = n_owners // 2
    nbits = pairs.bit_length() - 1
    acc = mine.astype(jnp.float32) + got.astype(jnp.float32)
    acc = acc.reshape((2,) * nbits + acc.shape[1:])
    dims = list(range(nbits - 1, -1, -1))
    for j in order:
        axis = dims.index(j)
        dims.pop(axis)
        bit = (chip >> j) & 1
        keep = lax.dynamic_index_in_dim(acc, bit, axis=axis, keepdims=False)
        send = lax.dynamic_index_in_dim(acc, 1 - bit, axis=axis, keepdims=False)
        recv = lax.ppermute(
            send.astype(jnp.bfloat16),
            "uv",
            _partner_pairs(n_owners, lambda i, j=j: ((i // 2) ^ (1 << j)) * 2 + i % 2),
        )
        acc = keep + recv.astype(jnp.float32)
    gridded = acc.astype(jnp.bfloat16)
    return lax.all_to_all(gridded, "chan", split_axis=1, concat_axis=2, tiled=True)


def _split_pairs(mine, got, chip, n_owners):
    pair_send = (mine.astype(jnp.float32) + got.astype(jnp.float32)).astype(jnp.bfloat16)
    own = lax.dynamic_index_in_dim(mine, chip, axis=0, keepdims=False).astype(
        jnp.float32
    ) + lax.dynamic_index_in_dim(got, chip, axis=0, keepdims=False).astype(jnp.float32)
    return _scatter_pairs(pair_send, own, chip, n_owners)


def _scatter_pairs(pair_send, own, chip, n_owners):
    pairs = n_owners // 2
    grid = own
    for d in range(1, pairs):
        if pairs & (pairs - 1):
            dest = lambda c, d=d: (c + d) % pairs
        else:
            dest = lambda c, d=d: c ^ d
        send = lax.dynamic_index_in_dim(pair_send, dest(chip), axis=0, keepdims=False)
        recv = lax.ppermute(
            send, "uv", _partner_pairs(n_owners, lambda i, dest=dest: dest(i // 2) * 2 + i % 2)
        )
        grid = grid + recv.astype(jnp.float32)
    gridded = grid.astype(jnp.bfloat16)
    return lax.all_to_all(gridded, "chan", split_axis=1, concat_axis=2, tiled=True)


def body(vis, row_cell, tap_weight, tap_offset, block_tile, tile_owner, galaxy):
    n_owners = lax.axis_size("uv")
    n_chan = lax.axis_size("chan")
    pairs = n_owners // 2
    me = lax.axis_index("uv")
    parity = me % 2
    chip = me // 2
    nblocks = block_tile.shape[0]
    slots_dev = galaxy.shape[0]
    chan_dev = vis.shape[2]

    rank_of_tile = tile_ranks(tile_owner, n_owners)
    owner = tile_owner[block_tile]
    rank = rank_of_tile[block_tile]
    slot = (owner % 2) * (pairs * slots_dev) + (owner // 2) * slots_dev + rank
    n_slots = n_owners * slots_dev
    pick = (jnp.arange(n_slots, dtype=jnp.int32)[:, None] == slot[None, :]).astype(jnp.bfloat16)
    pick2 = jnp.concatenate([pick, pick], axis=1)

    blocks = vis.reshape(nblocks, BR, 2, chan_dev)
    cells = row_cell.reshape(nblocks, BR)
    weights = jnp.transpose(tap_weight.reshape(KT, nblocks, BR), (1, 0, 2))
    matrix = kernel_matrix(cells, weights, tap_offset)
    table = delay_table()
    first = _gather_pair(blocks[:, :, 0, :], matrix, pick2, parity, chip, n_owners, slots_dev)
    second = _gather_pair(blocks[:, :, 1, :], matrix, pick2, parity, chip, n_owners, slots_dev)
    out = None
    pairs = n_owners // 2
    nbits = pairs.bit_length() - 1
    for k, (mine, got) in enumerate((first, second)):
        if pairs & (pairs - 1) or pairs == 1:
            piece = _split_pairs(mine, got, chip, n_owners)
        else:
            order = list(range(nbits)) if k == 0 else list(range(nbits - 1, -1, -1))
            piece = _halving(mine, got, chip, n_owners, order)
        count, cells_part = piece.shape[0], piece.shape[1]
        term = jnp.dot(
            piece.reshape(count * cells_part, CH),
            table[k * CH:(k + 1) * CH],
            preferred_element_type=jnp.float32,
        )
        out = term if out is None else out + term
    delay = out.reshape(count, cells_part, 2 * CH)
    galaxy_f = galaxy.astype(jnp.float32)
    product = delay[..., :CH] * galaxy_f[..., :CH] + delay[..., CH:] * galaxy_f[..., CH:]
    local_power = jnp.sum(product, axis=1)
    power = _allreduce_sum(local_power, "chan", n_chan) / jnp.float32(math.sqrt(TC))
    return (delay.astype(jnp.bfloat16), power)


def solution(mesh):
    return jax.shard_map(
        body,
        mesh=mesh,
        in_specs=(
            P("uv", None, "chan"),
            P("uv"),
            P(None, "uv"),
            P(),
            P("uv"),
            P(),
            P("uv", "chan", None),
        ),
        out_specs=(P("uv", "chan", None), P("uv", None)),
        check_vma=False,
    )
```

```python
import math

import jax
import jax.numpy as jnp
from jax import lax
from jax.sharding import PartitionSpec as P

CH = 1024
BR = 128
TC = 128
KT = 8


def tile_ranks(tile_owner, owners):
    onehot = (tile_owner[:, None] == jnp.arange(owners, dtype=jnp.int32)[None, :]).astype(jnp.int32)
    before = jnp.cumsum(onehot, axis=0) - onehot
    return jnp.sum(before * onehot, axis=1)


def kernel_matrix(cells, weights, tap_offset):
    positions = jnp.arange(TC, dtype=jnp.int32)
    total = jnp.zeros(cells.shape[:-1] + (TC, cells.shape[-1]), jnp.float32)
    for k in range(KT):
        target = cells + tap_offset[k]
        hit = target[..., None, :] == positions[:, None]
        total = total + jnp.where(
            hit, weights[..., k, :].astype(jnp.float32)[..., None, :], jnp.float32(0.0)
        )
    return total.astype(jnp.bfloat16)


def delay_table():
    freq = jnp.arange(CH, dtype=jnp.int32)
    phase = (freq[:, None] * freq[None, :] % CH).astype(jnp.float32) * jnp.float32(
        2.0 * math.pi / CH
    )
    cosine = jnp.cos(phase)
    sine = jnp.sin(phase)
    x = freq.astype(jnp.float32) * jnp.float32(2.0 * math.pi / CH)
    taper = 0.35875 - 0.48829 * jnp.cos(x) + 0.14128 * jnp.cos(2.0 * x) - 0.01168 * jnp.cos(3.0 * x)
    scale = (taper / jnp.float32(math.sqrt(CH)))[:, None]
    upper = jnp.concatenate([cosine * scale, -sine * scale], axis=1)
    lower = jnp.concatenate([sine * scale, cosine * scale], axis=1)
    return jnp.concatenate([upper, lower], axis=0).astype(jnp.bfloat16)


def _partner_pairs(n, fn):
    return [(i, fn(i)) for i in range(n)]


def _allreduce_sum(x, axis, n):
    if n & (n - 1):
        return lax.psum(x, axis)
    d = 1
    while d < n:
        x = x + lax.ppermute(x, axis, _partner_pairs(n, lambda i, d=d: i ^ d))
        d *= 2
    return x


def _gather_pair(part, matrix, pick2, parity, chip, n_owners, slots_dev):
    pairs = n_owners // 2
    contrib = jnp.einsum("bcr,brf->bcf", matrix, part, preferred_element_type=jnp.float32)
    high = contrib.astype(jnp.bfloat16)
    low = (contrib - high.astype(jnp.float32)).astype(jnp.bfloat16)
    partial = jnp.einsum(
        "sb,bcf->scf",
        pick2,
        jnp.concatenate([high, low], axis=0),
        preferred_element_type=jnp.float32,
    ).astype(jnp.bfloat16)
    partial = partial.reshape((2, pairs, slots_dev) + partial.shape[1:])

    mine = lax.dynamic_index_in_dim(partial, parity, axis=0, keepdims=False)
    other = lax.dynamic_index_in_dim(partial, 1 - parity, axis=0, keepdims=False)
    got = lax.ppermute(other, "uv", _partner_pairs(n_owners, lambda i: i ^ 1))
    pair_send = (mine.astype(jnp.float32) + got.astype(jnp.float32)).astype(jnp.bfloat16)
    own = lax.dynamic_index_in_dim(mine, chip, axis=0, keepdims=False).astype(
        jnp.float32
    ) + lax.dynamic_index_in_dim(got, chip, axis=0, keepdims=False).astype(jnp.float32)
    return pair_send, own


def _scatter_pairs(pair_send, own, chip, n_owners):
    pairs = n_owners // 2
    grid = own
    for d in range(1, pairs):
        if pairs & (pairs - 1):
            dest = lambda c, d=d: (c + d) % pairs
        else:
            dest = lambda c, d=d: c ^ d
        send = lax.dynamic_index_in_dim(pair_send, dest(chip), axis=0, keepdims=False)
        recv = lax.ppermute(
            send, "uv", _partner_pairs(n_owners, lambda i, dest=dest: dest(i // 2) * 2 + i % 2)
        )
        grid = grid + recv.astype(jnp.float32)
    gridded = grid.astype(jnp.bfloat16)
    return lax.all_to_all(gridded, "chan", split_axis=1, concat_axis=2, tiled=True)


def body(vis, row_cell, tap_weight, tap_offset, block_tile, tile_owner, galaxy):
    n_owners = lax.axis_size("uv")
    n_chan = lax.axis_size("chan")
    pairs = n_owners // 2
    me = lax.axis_index("uv")
    parity = me % 2
    chip = me // 2
    nblocks = block_tile.shape[0]
    slots_dev = galaxy.shape[0]
    chan_dev = vis.shape[2]

    rank_of_tile = tile_ranks(tile_owner, n_owners)
    owner = tile_owner[block_tile]
    rank = rank_of_tile[block_tile]
    slot = (owner % 2) * (pairs * slots_dev) + (owner // 2) * slots_dev + rank
    n_slots = n_owners * slots_dev
    pick = (jnp.arange(n_slots, dtype=jnp.int32)[:, None] == slot[None, :]).astype(jnp.bfloat16)
    pick2 = jnp.concatenate([pick, pick], axis=1)

    blocks = vis.reshape(nblocks, BR, 2, chan_dev)
    cells = row_cell.reshape(nblocks, BR)
    weights = jnp.transpose(tap_weight.reshape(KT, nblocks, BR), (1, 0, 2))
    matrix = kernel_matrix(cells, weights, tap_offset)
    table = delay_table()
    first = _gather_pair(blocks[:, :, 0, :], matrix, pick2, parity, chip, n_owners, slots_dev)
    second = _gather_pair(blocks[:, :, 1, :], matrix, pick2, parity, chip, n_owners, slots_dev)
    table, second = lax.optimization_barrier((table, second))
    out = None
    for k, (pair_send, own) in enumerate((first, second)):
        piece = _scatter_pairs(pair_send, own, chip, n_owners)
        count, cells_part = piece.shape[0], piece.shape[1]
        term = jnp.dot(
            piece.reshape(count * cells_part, CH),
            table[k * CH:(k + 1) * CH],
            preferred_element_type=jnp.float32,
        )
        out = term if out is None else out + term
    delay = out.reshape(count, cells_part, 2 * CH)
    galaxy_f = galaxy.astype(jnp.float32)
    product = delay[..., :CH] * galaxy_f[..., :CH] + delay[..., CH:] * galaxy_f[..., CH:]
    local_power = jnp.sum(product, axis=1)
    power = _allreduce_sum(local_power, "chan", n_chan) / jnp.float32(math.sqrt(TC))
    return (delay.astype(jnp.bfloat16), power)


def solution(mesh):
    return jax.shard_map(
        body,
        mesh=mesh,
        in_specs=(
            P("uv", None, "chan"),
            P("uv"),
            P(None, "uv"),
            P(),
            P("uv"),
            P(),
            P("uv", "chan", None),
        ),
        out_specs=(P("uv", "chan", None), P("uv", None)),
        check_vma=False,
    )
```

```python
import math

import jax
import jax.numpy as jnp
from jax import lax
from jax.sharding import PartitionSpec as P

CH = 1024
BR = 128
TC = 128
KT = 8


def tile_ranks(tile_owner, owners):
    onehot = (tile_owner[:, None] == jnp.arange(owners, dtype=jnp.int32)[None, :]).astype(jnp.int32)
    before = jnp.cumsum(onehot, axis=0) - onehot
    return jnp.sum(before * onehot, axis=1)


def kernel_matrix(cells, weights, tap_offset):
    positions = jnp.arange(TC, dtype=jnp.int32)
    total = jnp.zeros(cells.shape[:-1] + (TC, cells.shape[-1]), jnp.float32)
    for k in range(KT):
        target = cells + tap_offset[k]
        hit = target[..., None, :] == positions[:, None]
        total = total + jnp.where(
            hit, weights[..., k, :].astype(jnp.float32)[..., None, :], jnp.float32(0.0)
        )
    return total.astype(jnp.bfloat16)


def delay_table():
    freq = jnp.arange(CH, dtype=jnp.int32)
    phase = (freq[:, None] * freq[None, :] % CH).astype(jnp.float32) * jnp.float32(
        2.0 * math.pi / CH
    )
    cosine = jnp.cos(phase)
    sine = jnp.sin(phase)
    x = freq.astype(jnp.float32) * jnp.float32(2.0 * math.pi / CH)
    taper = 0.35875 - 0.48829 * jnp.cos(x) + 0.14128 * jnp.cos(2.0 * x) - 0.01168 * jnp.cos(3.0 * x)
    scale = (taper / jnp.float32(math.sqrt(CH)))[:, None]
    upper = jnp.concatenate([cosine * scale, -sine * scale], axis=1)
    lower = jnp.concatenate([sine * scale, cosine * scale], axis=1)
    return jnp.concatenate([upper, lower], axis=0).astype(jnp.bfloat16)


def _partner_pairs(n, fn):
    return [(i, fn(i)) for i in range(n)]


def _allreduce_sum(x, axis, n):
    if n & (n - 1):
        return lax.psum(x, axis)
    d = 1
    while d < n:
        x = x + lax.ppermute(x, axis, _partner_pairs(n, lambda i, d=d: i ^ d))
        d *= 2
    return x


def _gather_pair(part, matrix, pick2, parity, chip, n_owners, slots_dev):
    pairs = n_owners // 2
    contrib = jnp.einsum("bcr,brf->bcf", matrix, part, preferred_element_type=jnp.float32)
    high = contrib.astype(jnp.bfloat16)
    low = (contrib - high.astype(jnp.float32)).astype(jnp.bfloat16)
    partial = jnp.einsum(
        "sb,bcf->scf",
        pick2,
        jnp.concatenate([high, low], axis=0),
        preferred_element_type=jnp.float32,
    ).astype(jnp.bfloat16)
    partial = partial.reshape((2, pairs, slots_dev) + partial.shape[1:])

    mine = lax.dynamic_index_in_dim(partial, parity, axis=0, keepdims=False)
    other = lax.dynamic_index_in_dim(partial, 1 - parity, axis=0, keepdims=False)
    got = lax.ppermute(other, "uv", _partner_pairs(n_owners, lambda i: i ^ 1))
    pair_send = (mine.astype(jnp.float32) + got.astype(jnp.float32)).astype(jnp.bfloat16)
    own = lax.dynamic_index_in_dim(mine, chip, axis=0, keepdims=False).astype(
        jnp.float32
    ) + lax.dynamic_index_in_dim(got, chip, axis=0, keepdims=False).astype(jnp.float32)
    return pair_send, own


def _scatter_pairs(pair_send, own, chip, n_owners):
    pairs = n_owners // 2
    grid = own
    for d in range(1, pairs):
        if pairs & (pairs - 1):
            dest = lambda c, d=d: (c + d) % pairs
        else:
            dest = lambda c, d=d: c ^ d
        send = lax.dynamic_index_in_dim(pair_send, dest(chip), axis=0, keepdims=False)
        recv = lax.ppermute(
            send, "uv", _partner_pairs(n_owners, lambda i, dest=dest: dest(i // 2) * 2 + i % 2)
        )
        grid = grid + recv.astype(jnp.float32)
    return grid.astype(jnp.bfloat16)


def _chan_delay(gridded, table_half, n_chan):
    me = lax.axis_index("chan")
    cells_part = gridded.shape[1] // n_chan
    width = gridded.shape[2]
    out = None
    for d in range(n_chan):
        dest = (me + d) % n_chan
        send = lax.dynamic_slice_in_dim(gridded, dest * cells_part, cells_part, axis=1)
        if d == 0:
            recv = send
        else:
            recv = lax.ppermute(send, "chan", [(i, (i + d) % n_chan) for i in range(n_chan)])
        src = (me - d) % n_chan
        rows = lax.dynamic_slice_in_dim(table_half, src * width, width, axis=0)
        term = jnp.dot(recv.reshape(-1, width), rows, preferred_element_type=jnp.float32)
        out = term if out is None else out + term
    return out


def body(vis, row_cell, tap_weight, tap_offset, block_tile, tile_owner, galaxy):
    n_owners = lax.axis_size("uv")
    n_chan = lax.axis_size("chan")
    pairs = n_owners // 2
    me = lax.axis_index("uv")
    parity = me % 2
    chip = me // 2
    nblocks = block_tile.shape[0]
    slots_dev = galaxy.shape[0]
    chan_dev = vis.shape[2]

    rank_of_tile = tile_ranks(tile_owner, n_owners)
    owner = tile_owner[block_tile]
    rank = rank_of_tile[block_tile]
    slot = (owner % 2) * (pairs * slots_dev) + (owner // 2) * slots_dev + rank
    n_slots = n_owners * slots_dev
    pick = (jnp.arange(n_slots, dtype=jnp.int32)[:, None] == slot[None, :]).astype(jnp.bfloat16)
    pick2 = jnp.concatenate([pick, pick], axis=1)

    blocks = vis.reshape(nblocks, BR, 2, chan_dev)
    cells = row_cell.reshape(nblocks, BR)
    weights = jnp.transpose(tap_weight.reshape(KT, nblocks, BR), (1, 0, 2))
    matrix = kernel_matrix(cells, weights, tap_offset)
    table = delay_table()
    first = _gather_pair(blocks[:, :, 0, :], matrix, pick2, parity, chip, n_owners, slots_dev)
    second = _gather_pair(blocks[:, :, 1, :], matrix, pick2, parity, chip, n_owners, slots_dev)
    table, second = lax.optimization_barrier((table, second))
    out = None
    for k, (pair_send, own) in enumerate((first, second)):
        gridded = _scatter_pairs(pair_send, own, chip, n_owners)
        term = _chan_delay(gridded, table[k * CH:(k + 1) * CH], n_chan)
        out = term if out is None else out + term
    count, cells_part = slots_dev, TC // n_chan
    delay = out.reshape(count, cells_part, 2 * CH)
    galaxy_f = galaxy.astype(jnp.float32)
    product = delay[..., :CH] * galaxy_f[..., :CH] + delay[..., CH:] * galaxy_f[..., CH:]
    local_power = jnp.sum(product, axis=1)
    power = _allreduce_sum(local_power, "chan", n_chan) / jnp.float32(math.sqrt(TC))
    return (delay.astype(jnp.bfloat16), power)


def solution(mesh):
    return jax.shard_map(
        body,
        mesh=mesh,
        in_specs=(
            P("uv", None, "chan"),
            P("uv"),
            P(None, "uv"),
            P(),
            P("uv"),
            P(),
            P("uv", "chan", None),
        ),
        out_specs=(P("uv", "chan", None), P("uv", None)),
        check_vma=False,
    )
```

```python
import math

import jax
import jax.numpy as jnp
from jax import lax
from jax.sharding import PartitionSpec as P

CH = 1024
BR = 128
TC = 128
KT = 8


def tile_ranks(tile_owner, owners):
    onehot = (tile_owner[:, None] == jnp.arange(owners, dtype=jnp.int32)[None, :]).astype(jnp.int32)
    before = jnp.cumsum(onehot, axis=0) - onehot
    return jnp.sum(before * onehot, axis=1)


def kernel_matrix(cells, weights, tap_offset):
    positions = jnp.arange(TC, dtype=jnp.int32)
    total = jnp.zeros(cells.shape[:-1] + (TC, cells.shape[-1]), jnp.float32)
    for k in range(KT):
        target = cells + tap_offset[k]
        hit = target[..., None, :] == positions[:, None]
        total = total + jnp.where(
            hit, weights[..., k, :].astype(jnp.float32)[..., None, :], jnp.float32(0.0)
        )
    return total.astype(jnp.bfloat16)


def delay_parts():
    freq = jnp.arange(CH, dtype=jnp.int32)
    phase = (freq[:, None] * freq[None, :] % CH).astype(jnp.float32) * jnp.float32(
        2.0 * math.pi / CH
    )
    cosine = jnp.cos(phase)
    sine = jnp.sin(phase)
    x = freq.astype(jnp.float32) * jnp.float32(2.0 * math.pi / CH)
    taper = 0.35875 - 0.48829 * jnp.cos(x) + 0.14128 * jnp.cos(2.0 * x) - 0.01168 * jnp.cos(3.0 * x)
    scale = (taper / jnp.float32(math.sqrt(CH)))[:, None]
    return (cosine * scale).astype(jnp.bfloat16), (sine * scale).astype(jnp.bfloat16)


def _partner_pairs(n, fn):
    return [(i, fn(i)) for i in range(n)]


def _allreduce_sum(x, axis, n):
    if n & (n - 1):
        return lax.psum(x, axis)
    d = 1
    while d < n:
        x = x + lax.ppermute(x, axis, _partner_pairs(n, lambda i, d=d: i ^ d))
        d *= 2
    return x


def _gather_pair(part, matrix, pick2, parity, chip, n_owners, slots_dev):
    pairs = n_owners // 2
    contrib = jnp.einsum("bcr,brf->bcf", matrix, part, preferred_element_type=jnp.float32)
    high = contrib.astype(jnp.bfloat16)
    low = (contrib - high.astype(jnp.float32)).astype(jnp.bfloat16)
    partial = jnp.einsum(
        "sb,bcf->scf",
        pick2,
        jnp.concatenate([high, low], axis=0),
        preferred_element_type=jnp.float32,
    ).astype(jnp.bfloat16)
    partial = partial.reshape((2, pairs, slots_dev) + partial.shape[1:])

    mine = lax.dynamic_index_in_dim(partial, parity, axis=0, keepdims=False)
    other = lax.dynamic_index_in_dim(partial, 1 - parity, axis=0, keepdims=False)
    got = lax.ppermute(other, "uv", _partner_pairs(n_owners, lambda i: i ^ 1))
    pair_send = (mine.astype(jnp.float32) + got.astype(jnp.float32)).astype(jnp.bfloat16)
    own = lax.dynamic_index_in_dim(mine, chip, axis=0, keepdims=False).astype(
        jnp.float32
    ) + lax.dynamic_index_in_dim(got, chip, axis=0, keepdims=False).astype(jnp.float32)
    return pair_send, own


def _scatter_pairs(pair_send, own, chip, n_owners):
    pairs = n_owners // 2
    grid = own
    for d in range(1, pairs):
        if pairs & (pairs - 1):
            dest = lambda c, d=d: (c + d) % pairs
        else:
            dest = lambda c, d=d: c ^ d
        send = lax.dynamic_index_in_dim(pair_send, dest(chip), axis=0, keepdims=False)
        recv = lax.ppermute(
            send, "uv", _partner_pairs(n_owners, lambda i, dest=dest: dest(i // 2) * 2 + i % 2)
        )
        grid = grid + recv.astype(jnp.float32)
    gridded = grid.astype(jnp.bfloat16)
    return lax.all_to_all(gridded, "chan", split_axis=1, concat_axis=2, tiled=True)


def body(vis, row_cell, tap_weight, tap_offset, block_tile, tile_owner, galaxy):
    n_owners = lax.axis_size("uv")
    n_chan = lax.axis_size("chan")
    pairs = n_owners // 2
    me = lax.axis_index("uv")
    parity = me % 2
    chip = me // 2
    nblocks = block_tile.shape[0]
    slots_dev = galaxy.shape[0]
    chan_dev = vis.shape[2]

    rank_of_tile = tile_ranks(tile_owner, n_owners)
    owner = tile_owner[block_tile]
    rank = rank_of_tile[block_tile]
    slot = (owner % 2) * (pairs * slots_dev) + (owner // 2) * slots_dev + rank
    n_slots = n_owners * slots_dev
    pick = (jnp.arange(n_slots, dtype=jnp.int32)[:, None] == slot[None, :]).astype(jnp.bfloat16)
    pick2 = jnp.concatenate([pick, pick], axis=1)

    blocks = vis.reshape(nblocks, BR, 2, chan_dev)
    cells = row_cell.reshape(nblocks, BR)
    weights = jnp.transpose(tap_weight.reshape(KT, nblocks, BR), (1, 0, 2))
    matrix = kernel_matrix(cells, weights, tap_offset)
    cos_part, sin_part = delay_parts()
    first = _gather_pair(blocks[:, :, 0, :], matrix, pick2, parity, chip, n_owners, slots_dev)
    second = _gather_pair(blocks[:, :, 1, :], matrix, pick2, parity, chip, n_owners, slots_dev)
    cos_part, sin_part, second = lax.optimization_barrier((cos_part, sin_part, second))
    flat = []
    for pair_send, own in (first, second):
        piece = _scatter_pairs(pair_send, own, chip, n_owners)
        count, cells_part = piece.shape[0], piece.shape[1]
        flat.append(piece.reshape(count * cells_part, CH))

    def mul(a, b):
        return jnp.dot(a, b, preferred_element_type=jnp.float32)

    left = mul(flat[0], cos_part) + mul(flat[1], sin_part)
    right = mul(flat[1], cos_part) - mul(flat[0], sin_part)
    out = jnp.concatenate([left, right], axis=1)
    delay = out.reshape(count, cells_part, 2 * CH)
    galaxy_f = galaxy.astype(jnp.float32)
    product = delay[..., :CH] * galaxy_f[..., :CH] + delay[..., CH:] * galaxy_f[..., CH:]
    local_power = jnp.sum(product, axis=1)
    power = _allreduce_sum(local_power, "chan", n_chan) / jnp.float32(math.sqrt(TC))
    return (delay.astype(jnp.bfloat16), power)


def solution(mesh):
    return jax.shard_map(
        body,
        mesh=mesh,
        in_specs=(
            P("uv", None, "chan"),
            P("uv"),
            P(None, "uv"),
            P(),
            P("uv"),
            P(),
            P("uv", "chan", None),
        ),
        out_specs=(P("uv", "chan", None), P("uv", None)),
        check_vma=False,
    )
```

```python
import math

import jax
import jax.numpy as jnp
from jax import lax
from jax.sharding import PartitionSpec as P

CH = 1024
BR = 128
TC = 128
KT = 8


def tile_ranks(tile_owner, owners):
    onehot = (tile_owner[:, None] == jnp.arange(owners, dtype=jnp.int32)[None, :]).astype(jnp.int32)
    before = jnp.cumsum(onehot, axis=0) - onehot
    return jnp.sum(before * onehot, axis=1)


def kernel_matrix(cells, weights, tap_offset):
    positions = jnp.arange(TC, dtype=jnp.int32)
    total = jnp.zeros(cells.shape[:-1] + (TC, cells.shape[-1]), jnp.float32)
    for k in range(KT):
        target = cells + tap_offset[k]
        hit = target[..., None, :] == positions[:, None]
        total = total + jnp.where(
            hit, weights[..., k, :].astype(jnp.float32)[..., None, :], jnp.float32(0.0)
        )
    return total.astype(jnp.bfloat16)


def delay_table():
    freq = jnp.arange(CH, dtype=jnp.int32)
    phase = (freq[:, None] * freq[None, :] % CH).astype(jnp.float32) * jnp.float32(
        2.0 * math.pi / CH
    )
    cosine = jnp.cos(phase)
    sine = jnp.sin(phase)
    x = freq.astype(jnp.float32) * jnp.float32(2.0 * math.pi / CH)
    taper = 0.35875 - 0.48829 * jnp.cos(x) + 0.14128 * jnp.cos(2.0 * x) - 0.01168 * jnp.cos(3.0 * x)
    scale = (taper / jnp.float32(math.sqrt(CH)))[:, None]
    upper = jnp.concatenate([cosine * scale, -sine * scale], axis=1)
    lower = jnp.concatenate([sine * scale, cosine * scale], axis=1)
    return jnp.concatenate([upper, lower], axis=0).astype(jnp.bfloat16)


def _partner_pairs(n, fn):
    return [(i, fn(i)) for i in range(n)]


def _allreduce_sum(x, axis, n):
    if n & (n - 1):
        return lax.psum(x, axis)
    d = 1
    while d < n:
        x = x + lax.ppermute(x, axis, _partner_pairs(n, lambda i, d=d: i ^ d))
        d *= 2
    return x


def _gather_pair(part, matrix, pick2, parity, chip, n_owners, slots_dev, after=None):
    pairs = n_owners // 2
    contrib = jnp.einsum("bcr,brf->bcf", matrix, part, preferred_element_type=jnp.float32)
    high = contrib.astype(jnp.bfloat16)
    low = (contrib - high.astype(jnp.float32)).astype(jnp.bfloat16)
    partial = jnp.einsum(
        "sb,bcf->scf",
        pick2,
        jnp.concatenate([high, low], axis=0),
        preferred_element_type=jnp.float32,
    ).astype(jnp.bfloat16)
    partial = partial.reshape((2, pairs, slots_dev) + partial.shape[1:])

    mine = lax.dynamic_index_in_dim(partial, parity, axis=0, keepdims=False)
    other = lax.dynamic_index_in_dim(partial, 1 - parity, axis=0, keepdims=False)
    if after is not None:
        other, _ = lax.optimization_barrier((other, after))
    got = lax.ppermute(other, "uv", _partner_pairs(n_owners, lambda i: i ^ 1))
    pair_send = (mine.astype(jnp.float32) + got.astype(jnp.float32)).astype(jnp.bfloat16)
    own = lax.dynamic_index_in_dim(mine, chip, axis=0, keepdims=False).astype(
        jnp.float32
    ) + lax.dynamic_index_in_dim(got, chip, axis=0, keepdims=False).astype(jnp.float32)
    return pair_send, own


def _scatter_pairs(pair_send, own, chip, n_owners):
    pairs = n_owners // 2
    grid = own
    for d in range(1, pairs):
        if pairs & (pairs - 1):
            dest = lambda c, d=d: (c + d) % pairs
        else:
            dest = lambda c, d=d: c ^ d
        send = lax.dynamic_index_in_dim(pair_send, dest(chip), axis=0, keepdims=False)
        recv = lax.ppermute(
            send, "uv", _partner_pairs(n_owners, lambda i, dest=dest: dest(i // 2) * 2 + i % 2)
        )
        grid = grid + recv.astype(jnp.float32)
    return grid.astype(jnp.bfloat16)


def body(vis, row_cell, tap_weight, tap_offset, block_tile, tile_owner, galaxy):
    n_owners = lax.axis_size("uv")
    n_chan = lax.axis_size("chan")
    pairs = n_owners // 2
    me = lax.axis_index("uv")
    parity = me % 2
    chip = me // 2
    nblocks = block_tile.shape[0]
    slots_dev = galaxy.shape[0]
    chan_dev = vis.shape[2]

    rank_of_tile = tile_ranks(tile_owner, n_owners)
    owner = tile_owner[block_tile]
    rank = rank_of_tile[block_tile]
    slot = (owner % 2) * (pairs * slots_dev) + (owner // 2) * slots_dev + rank
    n_slots = n_owners * slots_dev
    pick = (jnp.arange(n_slots, dtype=jnp.int32)[:, None] == slot[None, :]).astype(jnp.bfloat16)
    pick2 = jnp.concatenate([pick, pick], axis=1)

    width = 2 * chan_dev
    blocks = vis.reshape(nblocks, BR, width)
    cells = row_cell.reshape(nblocks, BR)
    weights = jnp.transpose(tap_weight.reshape(KT, nblocks, BR), (1, 0, 2))
    matrix = kernel_matrix(cells, weights, tap_offset)
    table = delay_table()
    cut = width - width // 4
    first = _gather_pair(blocks[:, :, :cut], matrix, pick2, parity, chip, n_owners, slots_dev)
    first_grid = _scatter_pairs(first[0], first[1], chip, n_owners)
    second = _gather_pair(
        blocks[:, :, cut:], matrix, pick2, parity, chip, n_owners, slots_dev, after=first_grid
    )
    table, first_grid = lax.optimization_barrier((table, first_grid))
    second_grid = _scatter_pairs(second[0], second[1], chip, n_owners)
    by_source = table.reshape(2, n_chan, chan_dev, 2 * CH).transpose(1, 0, 2, 3)
    by_source = by_source.reshape(n_chan, width, 2 * CH)
    out = None
    for gridded, lo, hi in ((first_grid, 0, cut), (second_grid, cut, width)):
        piece = lax.all_to_all(gridded, "chan", split_axis=1, concat_axis=2, tiled=True)
        count, cells_part = piece.shape[0], piece.shape[1]
        rows = by_source[:, lo:hi, :].reshape(n_chan * (hi - lo), 2 * CH)
        term = jnp.dot(
            piece.reshape(count * cells_part, n_chan * (hi - lo)),
            rows,
            preferred_element_type=jnp.float32,
        )
        out = term if out is None else out + term
    delay = out.reshape(count, cells_part, 2 * CH)
    galaxy_f = galaxy.astype(jnp.float32)
    product = delay[..., :CH] * galaxy_f[..., :CH] + delay[..., CH:] * galaxy_f[..., CH:]
    local_power = jnp.sum(product, axis=1)
    power = _allreduce_sum(local_power, "chan", n_chan) / jnp.float32(math.sqrt(TC))
    return (delay.astype(jnp.bfloat16), power)


def solution(mesh):
    return jax.shard_map(
        body,
        mesh=mesh,
        in_specs=(
            P("uv", None, "chan"),
            P("uv"),
            P(None, "uv"),
            P(),
            P("uv"),
            P(),
            P("uv", "chan", None),
        ),
        out_specs=(P("uv", "chan", None), P("uv", None)),
        check_vma=False,
    )
```

```python
import math

import jax
import jax.numpy as jnp
from jax import lax
from jax.sharding import PartitionSpec as P

CH = 1024
BR = 128
TC = 128
KT = 8


def tile_ranks(tile_owner, owners):
    onehot = (tile_owner[:, None] == jnp.arange(owners, dtype=jnp.int32)[None, :]).astype(jnp.int32)
    before = jnp.cumsum(onehot, axis=0) - onehot
    return jnp.sum(before * onehot, axis=1)


def kernel_matrix(cells, weights, tap_offset):
    positions = jnp.arange(TC, dtype=jnp.int32)
    total = jnp.zeros(cells.shape[:-1] + (TC, cells.shape[-1]), jnp.float32)
    for k in range(KT):
        target = cells + tap_offset[k]
        hit = target[..., None, :] == positions[:, None]
        total = total + jnp.where(
            hit, weights[..., k, :].astype(jnp.float32)[..., None, :], jnp.float32(0.0)
        )
    return total.astype(jnp.bfloat16)


def delay_table():
    freq = jnp.arange(CH, dtype=jnp.int32)
    phase = (freq[:, None] * freq[None, :] % CH).astype(jnp.float32) * jnp.float32(
        2.0 * math.pi / CH
    )
    cosine = jnp.cos(phase)
    sine = jnp.sin(phase)
    x = freq.astype(jnp.float32) * jnp.float32(2.0 * math.pi / CH)
    taper = 0.35875 - 0.48829 * jnp.cos(x) + 0.14128 * jnp.cos(2.0 * x) - 0.01168 * jnp.cos(3.0 * x)
    scale = (taper / jnp.float32(math.sqrt(CH)))[:, None]
    upper = jnp.concatenate([cosine * scale, -sine * scale], axis=1)
    lower = jnp.concatenate([sine * scale, cosine * scale], axis=1)
    return jnp.concatenate([upper, lower], axis=0).astype(jnp.bfloat16)


def _partner_pairs(n, fn):
    return [(i, fn(i)) for i in range(n)]


def _allreduce_sum(x, axis, n):
    if n & (n - 1):
        return lax.psum(x, axis)
    d = 1
    while d < n:
        x = x + lax.ppermute(x, axis, _partner_pairs(n, lambda i, d=d: i ^ d))
        d *= 2
    return x


def _gather_pair(part, matrix, pick2, parity, chip, n_owners, slots_dev):
    pairs = n_owners // 2
    contrib = jnp.einsum("bcr,brf->bcf", matrix, part, preferred_element_type=jnp.float32)
    high = contrib.astype(jnp.bfloat16)
    low = (contrib - high.astype(jnp.float32)).astype(jnp.bfloat16)
    partial = jnp.einsum(
        "sb,bcf->scf",
        pick2,
        jnp.concatenate([high, low], axis=0),
        preferred_element_type=jnp.float32,
    ).astype(jnp.bfloat16)
    partial = partial.reshape((2, pairs, slots_dev) + partial.shape[1:])

    mine = lax.dynamic_index_in_dim(partial, parity, axis=0, keepdims=False)
    other = lax.dynamic_index_in_dim(partial, 1 - parity, axis=0, keepdims=False)
    got = lax.ppermute(other, "uv", _partner_pairs(n_owners, lambda i: i ^ 1))
    pair_send = (mine.astype(jnp.float32) + got.astype(jnp.float32)).astype(jnp.bfloat16)
    own = lax.dynamic_index_in_dim(mine, chip, axis=0, keepdims=False).astype(
        jnp.float32
    ) + lax.dynamic_index_in_dim(got, chip, axis=0, keepdims=False).astype(jnp.float32)
    return pair_send, own


def _scatter_pairs(pair_send, own, chip, n_owners):
    pairs = n_owners // 2
    grid = own
    for d in range(1, pairs):
        if pairs & (pairs - 1):
            dest = lambda c, d=d: (c + d) % pairs
        else:
            dest = lambda c, d=d: c ^ d
        send = lax.dynamic_index_in_dim(pair_send, dest(chip), axis=0, keepdims=False)
        recv = lax.ppermute(
            send, "uv", _partner_pairs(n_owners, lambda i, dest=dest: dest(i // 2) * 2 + i % 2)
        )
        grid = grid + recv.astype(jnp.float32)
    gridded = grid.astype(jnp.bfloat16)
    return lax.all_to_all(gridded, "chan", split_axis=1, concat_axis=2, tiled=True)


def body(vis, row_cell, tap_weight, tap_offset, block_tile, tile_owner, galaxy):
    n_owners = lax.axis_size("uv")
    n_chan = lax.axis_size("chan")
    pairs = n_owners // 2
    me = lax.axis_index("uv")
    parity = me % 2
    chip = me // 2
    nblocks = block_tile.shape[0]
    slots_dev = galaxy.shape[0]
    chan_dev = vis.shape[2]

    rank_of_tile = tile_ranks(tile_owner, n_owners)
    owner = tile_owner[block_tile]
    rank = rank_of_tile[block_tile]
    slot = (owner % 2) * (pairs * slots_dev) + (owner // 2) * slots_dev + rank
    n_slots = n_owners * slots_dev
    pick = (jnp.arange(n_slots, dtype=jnp.int32)[:, None] == slot[None, :]).astype(jnp.bfloat16)
    pick2 = jnp.concatenate([pick, pick], axis=1)

    blocks = vis.reshape(nblocks, BR, 2, chan_dev)
    cells = row_cell.reshape(nblocks, BR)
    weights = jnp.transpose(tap_weight.reshape(KT, nblocks, BR), (1, 0, 2))
    matrix = kernel_matrix(cells, weights, tap_offset)
    table = delay_table()
    first = _gather_pair(blocks[:, :, 0, :], matrix, pick2, parity, chip, n_owners, slots_dev)
    second = _gather_pair(blocks[:, :, 1, :], matrix, pick2, parity, chip, n_owners, slots_dev)
    galaxy_f = galaxy.astype(jnp.float32)
    table, galaxy_f, second = lax.optimization_barrier((table, galaxy_f, second))
    out = None
    for k, (pair_send, own) in enumerate((first, second)):
        piece = _scatter_pairs(pair_send, own, chip, n_owners)
        count, cells_part = piece.shape[0], piece.shape[1]
        term = jnp.dot(
            piece.reshape(count * cells_part, CH),
            table[k * CH:(k + 1) * CH],
            preferred_element_type=jnp.float32,
        )
        out = term if out is None else out + term
    delay = out.reshape(count, cells_part, 2 * CH)
    product = delay[..., :CH] * galaxy_f[..., :CH] + delay[..., CH:] * galaxy_f[..., CH:]
    local_power = jnp.sum(product, axis=1)
    power = _allreduce_sum(local_power, "chan", n_chan) / jnp.float32(math.sqrt(TC))
    return (delay.astype(jnp.bfloat16), power)


def solution(mesh):
    return jax.shard_map(
        body,
        mesh=mesh,
        in_specs=(
            P("uv", None, "chan"),
            P("uv"),
            P(None, "uv"),
            P(),
            P("uv"),
            P(),
            P("uv", "chan", None),
        ),
        out_specs=(P("uv", "chan", None), P("uv", None)),
        check_vma=False,
    )
```

```python
import math

import jax
import jax.numpy as jnp
from jax import lax
from jax.sharding import PartitionSpec as P

CH = 1024
BR = 128
TC = 128
KT = 8


def tile_ranks(tile_owner, owners):
    onehot = (tile_owner[:, None] == jnp.arange(owners, dtype=jnp.int32)[None, :]).astype(jnp.int32)
    before = jnp.cumsum(onehot, axis=0) - onehot
    return jnp.sum(before * onehot, axis=1)


def kernel_matrix(cells, weights, tap_offset):
    positions = jnp.arange(TC, dtype=jnp.int32)
    total = jnp.zeros(cells.shape[:-1] + (TC, cells.shape[-1]), jnp.float32)
    for k in range(KT):
        target = cells + tap_offset[k]
        hit = target[..., None, :] == positions[:, None]
        total = total + jnp.where(
            hit, weights[..., k, :].astype(jnp.float32)[..., None, :], jnp.float32(0.0)
        )
    return total.astype(jnp.bfloat16)


def delay_table():
    freq = jnp.arange(CH, dtype=jnp.int32)
    phase = (freq[:, None] * freq[None, :] % CH).astype(jnp.float32) * jnp.float32(
        2.0 * math.pi / CH
    )
    cosine = jnp.cos(phase)
    sine = jnp.sin(phase)
    x = freq.astype(jnp.float32) * jnp.float32(2.0 * math.pi / CH)
    taper = 0.35875 - 0.48829 * jnp.cos(x) + 0.14128 * jnp.cos(2.0 * x) - 0.01168 * jnp.cos(3.0 * x)
    scale = (taper / jnp.float32(math.sqrt(CH)))[:, None]
    upper = jnp.concatenate([cosine * scale, -sine * scale], axis=1)
    lower = jnp.concatenate([sine * scale, cosine * scale], axis=1)
    return jnp.concatenate([upper, lower], axis=0).astype(jnp.bfloat16)


def _partner_pairs(n, fn):
    return [(i, fn(i)) for i in range(n)]


def _allreduce_sum(x, axis, n):
    if n & (n - 1):
        return lax.psum(x, axis)
    d = 1
    while d < n:
        x = x + lax.ppermute(x, axis, _partner_pairs(n, lambda i, d=d: i ^ d))
        d *= 2
    return x


def _gather_pair(part, matrix, pick, parity, chip, n_owners, slots_dev):
    pairs = n_owners // 2
    contrib = jnp.einsum("bcr,brf->bcf", matrix, part, preferred_element_type=jnp.float32)
    partial = jnp.einsum(
        "sb,bcf->scf",
        pick,
        contrib,
        precision=lax.Precision.HIGH,
        preferred_element_type=jnp.float32,
    ).astype(jnp.bfloat16)
    partial = partial.reshape((2, pairs, slots_dev) + partial.shape[1:])

    mine = lax.dynamic_index_in_dim(partial, parity, axis=0, keepdims=False)
    other = lax.dynamic_index_in_dim(partial, 1 - parity, axis=0, keepdims=False)
    got = lax.ppermute(other, "uv", _partner_pairs(n_owners, lambda i: i ^ 1))
    pair_send = (mine.astype(jnp.float32) + got.astype(jnp.float32)).astype(jnp.bfloat16)
    own = lax.dynamic_index_in_dim(mine, chip, axis=0, keepdims=False).astype(
        jnp.float32
    ) + lax.dynamic_index_in_dim(got, chip, axis=0, keepdims=False).astype(jnp.float32)
    return pair_send, own


def _scatter_pairs(pair_send, own, chip, n_owners):
    pairs = n_owners // 2
    grid = own
    for d in range(1, pairs):
        if pairs & (pairs - 1):
            dest = lambda c, d=d: (c + d) % pairs
        else:
            dest = lambda c, d=d: c ^ d
        send = lax.dynamic_index_in_dim(pair_send, dest(chip), axis=0, keepdims=False)
        recv = lax.ppermute(
            send, "uv", _partner_pairs(n_owners, lambda i, dest=dest: dest(i // 2) * 2 + i % 2)
        )
        grid = grid + recv.astype(jnp.float32)
    gridded = grid.astype(jnp.bfloat16)
    return lax.all_to_all(gridded, "chan", split_axis=1, concat_axis=2, tiled=True)


def body(vis, row_cell, tap_weight, tap_offset, block_tile, tile_owner, galaxy):
    n_owners = lax.axis_size("uv")
    n_chan = lax.axis_size("chan")
    pairs = n_owners // 2
    me = lax.axis_index("uv")
    parity = me % 2
    chip = me // 2
    nblocks = block_tile.shape[0]
    slots_dev = galaxy.shape[0]
    chan_dev = vis.shape[2]

    rank_of_tile = tile_ranks(tile_owner, n_owners)
    owner = tile_owner[block_tile]
    rank = rank_of_tile[block_tile]
    slot = (owner % 2) * (pairs * slots_dev) + (owner // 2) * slots_dev + rank
    n_slots = n_owners * slots_dev
    pick = (jnp.arange(n_slots, dtype=jnp.int32)[:, None] == slot[None, :]).astype(jnp.float32)

    blocks = vis.reshape(nblocks, BR, 2, chan_dev)
    cells = row_cell.reshape(nblocks, BR)
    weights = jnp.transpose(tap_weight.reshape(KT, nblocks, BR), (1, 0, 2))
    matrix = kernel_matrix(cells, weights, tap_offset)
    table = delay_table()
    first = _gather_pair(blocks[:, :, 0, :], matrix, pick, parity, chip, n_owners, slots_dev)
    second = _gather_pair(blocks[:, :, 1, :], matrix, pick, parity, chip, n_owners, slots_dev)
    galaxy_f = galaxy.astype(jnp.float32)
    table, galaxy_f, second = lax.optimization_barrier((table, galaxy_f, second))
    out = None
    for k, (pair_send, own) in enumerate((first, second)):
        piece = _scatter_pairs(pair_send, own, chip, n_owners)
        count, cells_part = piece.shape[0], piece.shape[1]
        term = jnp.dot(
            piece.reshape(count * cells_part, CH),
            table[k * CH:(k + 1) * CH],
            preferred_element_type=jnp.float32,
        )
        out = term if out is None else out + term
    delay = out.reshape(count, cells_part, 2 * CH)
    product = delay[..., :CH] * galaxy_f[..., :CH] + delay[..., CH:] * galaxy_f[..., CH:]
    local_power = jnp.sum(product, axis=1)
    power = _allreduce_sum(local_power, "chan", n_chan) / jnp.float32(math.sqrt(TC))
    return (delay.astype(jnp.bfloat16), power)


def solution(mesh):
    return jax.shard_map(
        body,
        mesh=mesh,
        in_specs=(
            P("uv", None, "chan"),
            P("uv"),
            P(None, "uv"),
            P(),
            P("uv"),
            P(),
            P("uv", "chan", None),
        ),
        out_specs=(P("uv", "chan", None), P("uv", None)),
        check_vma=False,
    )
```

```python
import math

import jax
import jax.numpy as jnp
from jax import lax
from jax.sharding import PartitionSpec as P

CH = 1024
BR = 128
TC = 128
KT = 8


def tile_ranks(tile_owner, owners):
    onehot = (tile_owner[:, None] == jnp.arange(owners, dtype=jnp.int32)[None, :]).astype(jnp.int32)
    before = jnp.cumsum(onehot, axis=0) - onehot
    return jnp.sum(before * onehot, axis=1)


def kernel_matrix(cells, weights, tap_offset):
    positions = jnp.arange(TC, dtype=jnp.int32)
    total = jnp.zeros(cells.shape[:-1] + (TC, cells.shape[-1]), jnp.float32)
    for k in range(KT):
        target = cells + tap_offset[k]
        hit = target[..., None, :] == positions[:, None]
        total = total + jnp.where(
            hit, weights[..., k, :].astype(jnp.float32)[..., None, :], jnp.float32(0.0)
        )
    return total.astype(jnp.bfloat16)


def delay_table():
    freq = jnp.arange(CH, dtype=jnp.int32)
    phase = (freq[:, None] * freq[None, :] % CH).astype(jnp.float32) * jnp.float32(
        2.0 * math.pi / CH
    )
    cosine = jnp.cos(phase)
    sine = jnp.sin(phase)
    x = freq.astype(jnp.float32) * jnp.float32(2.0 * math.pi / CH)
    taper = 0.35875 - 0.48829 * jnp.cos(x) + 0.14128 * jnp.cos(2.0 * x) - 0.01168 * jnp.cos(3.0 * x)
    scale = (taper / jnp.float32(math.sqrt(CH)))[:, None]
    upper = jnp.concatenate([cosine * scale, -sine * scale], axis=1)
    lower = jnp.concatenate([sine * scale, cosine * scale], axis=1)
    return jnp.concatenate([upper, lower], axis=0).astype(jnp.bfloat16)


def _partner_pairs(n, fn):
    return [(i, fn(i)) for i in range(n)]


def _allreduce_sum(x, axis, n):
    if n & (n - 1):
        return lax.psum(x, axis)
    d = 1
    while d < n:
        x = x + lax.ppermute(x, axis, _partner_pairs(n, lambda i, d=d: i ^ d))
        d *= 2
    return x


def _gather_pair(part, matrix, pick2, parity, chip, n_owners, slots_dev):
    pairs = n_owners // 2
    contrib = jnp.einsum("bcr,brf->bcf", matrix, part, preferred_element_type=jnp.float32)
    high = contrib.astype(jnp.bfloat16)
    low = (contrib - high.astype(jnp.float32)).astype(jnp.bfloat16)
    partial = jnp.einsum(
        "sb,bcf->scf",
        pick2,
        jnp.concatenate([high, low], axis=0),
        preferred_element_type=jnp.float32,
    ).astype(jnp.bfloat16)
    partial = partial.reshape((2, pairs, slots_dev) + partial.shape[1:])

    mine = lax.dynamic_index_in_dim(partial, parity, axis=0, keepdims=False)
    other = lax.dynamic_index_in_dim(partial, 1 - parity, axis=0, keepdims=False)
    got = lax.ppermute(other, "uv", _partner_pairs(n_owners, lambda i: i ^ 1))
    pair_send = (mine.astype(jnp.float32) + got.astype(jnp.float32)).astype(jnp.bfloat16)
    own = lax.dynamic_index_in_dim(mine, chip, axis=0, keepdims=False).astype(
        jnp.float32
    ) + lax.dynamic_index_in_dim(got, chip, axis=0, keepdims=False).astype(jnp.float32)
    return pair_send, own


def _scatter_pairs(pair_send, own, chip, n_owners):
    pairs = n_owners // 2
    grid = own
    for d in range(1, pairs):
        if pairs & (pairs - 1):
            dest = lambda c, d=d: (c + d) % pairs
        else:
            dest = lambda c, d=d: c ^ d
        send = lax.dynamic_index_in_dim(pair_send, dest(chip), axis=0, keepdims=False)
        recv = lax.ppermute(
            send, "uv", _partner_pairs(n_owners, lambda i, dest=dest: dest(i // 2) * 2 + i % 2)
        )
        grid = grid + recv.astype(jnp.float32)
    return grid.astype(jnp.bfloat16)


def _chan_delay(gridded, table_half, n_chan):
    me = lax.axis_index("chan")
    cells_part = gridded.shape[1] // n_chan
    width = gridded.shape[2]
    out = None
    for d in range(n_chan):
        dest = (me + d) % n_chan
        send = lax.dynamic_slice_in_dim(gridded, dest * cells_part, cells_part, axis=1)
        if d == 0:
            recv = send
        else:
            recv = lax.ppermute(send, "chan", [(i, (i + d) % n_chan) for i in range(n_chan)])
        src = (me - d) % n_chan
        rows = lax.dynamic_slice_in_dim(table_half, src * width, width, axis=0)
        term = jnp.dot(recv.reshape(-1, width), rows, preferred_element_type=jnp.float32)
        out = term if out is None else out + term
    return out


def body(vis, row_cell, tap_weight, tap_offset, block_tile, tile_owner, galaxy):
    n_owners = lax.axis_size("uv")
    n_chan = lax.axis_size("chan")
    pairs = n_owners // 2
    me = lax.axis_index("uv")
    parity = me % 2
    chip = me // 2
    nblocks = block_tile.shape[0]
    slots_dev = galaxy.shape[0]
    chan_dev = vis.shape[2]

    rank_of_tile = tile_ranks(tile_owner, n_owners)
    owner = tile_owner[block_tile]
    rank = rank_of_tile[block_tile]
    slot = (owner % 2) * (pairs * slots_dev) + (owner // 2) * slots_dev + rank
    n_slots = n_owners * slots_dev
    pick = (jnp.arange(n_slots, dtype=jnp.int32)[:, None] == slot[None, :]).astype(jnp.bfloat16)
    pick2 = jnp.concatenate([pick, pick], axis=1)

    blocks = vis.reshape(nblocks, BR, 2, chan_dev)
    cells = row_cell.reshape(nblocks, BR)
    weights = jnp.transpose(tap_weight.reshape(KT, nblocks, BR), (1, 0, 2))
    matrix = kernel_matrix(cells, weights, tap_offset)
    table = delay_table()
    first = _gather_pair(blocks[:, :, 0, :], matrix, pick2, parity, chip, n_owners, slots_dev)
    second = _gather_pair(blocks[:, :, 1, :], matrix, pick2, parity, chip, n_owners, slots_dev)
    table, second = lax.optimization_barrier((table, second))
    out = None
    for k, (pair_send, own) in enumerate((first, second)):
        gridded = _scatter_pairs(pair_send, own, chip, n_owners)
        half = table[k * CH:(k + 1) * CH]
        if k == 0:
            piece = lax.all_to_all(gridded, "chan", split_axis=1, concat_axis=2, tiled=True)
            term = jnp.dot(
                piece.reshape(-1, CH), half, preferred_element_type=jnp.float32
            )
        else:
            term = _chan_delay(gridded, half, n_chan)
        out = term if out is None else out + term
    count, cells_part = slots_dev, TC // n_chan
    delay = out.reshape(count, cells_part, 2 * CH)
    galaxy_f = galaxy.astype(jnp.float32)
    product = delay[..., :CH] * galaxy_f[..., :CH] + delay[..., CH:] * galaxy_f[..., CH:]
    local_power = jnp.sum(product, axis=1)
    power = _allreduce_sum(local_power, "chan", n_chan) / jnp.float32(math.sqrt(TC))
    return (delay.astype(jnp.bfloat16), power)


def solution(mesh):
    return jax.shard_map(
        body,
        mesh=mesh,
        in_specs=(
            P("uv", None, "chan"),
            P("uv"),
            P(None, "uv"),
            P(),
            P("uv"),
            P(),
            P("uv", "chan", None),
        ),
        out_specs=(P("uv", "chan", None), P("uv", None)),
        check_vma=False,
    )
```

```python
import math

import jax
import jax.numpy as jnp
from jax import lax
from jax.sharding import PartitionSpec as P

CH = 1024
BR = 128
TC = 128
KT = 8


def tile_ranks(tile_owner, owners):
    onehot = (tile_owner[:, None] == jnp.arange(owners, dtype=jnp.int32)[None, :]).astype(jnp.int32)
    before = jnp.cumsum(onehot, axis=0) - onehot
    return jnp.sum(before * onehot, axis=1)


def kernel_matrix(cells, weights, tap_offset):
    positions = jnp.arange(TC, dtype=jnp.int32)
    total = jnp.zeros(cells.shape[:-1] + (TC, cells.shape[-1]), jnp.float32)
    for k in range(KT):
        target = cells + tap_offset[k]
        hit = target[..., None, :] == positions[:, None]
        total = total + jnp.where(
            hit, weights[..., k, :].astype(jnp.float32)[..., None, :], jnp.float32(0.0)
        )
    return total.astype(jnp.bfloat16)


def delay_table():
    freq = jnp.arange(CH, dtype=jnp.int32)
    phase = (freq[:, None] * freq[None, :] % CH).astype(jnp.float32) * jnp.float32(
        2.0 * math.pi / CH
    )
    cosine = jnp.cos(phase)
    sine = jnp.sin(phase)
    x = freq.astype(jnp.float32) * jnp.float32(2.0 * math.pi / CH)
    taper = 0.35875 - 0.48829 * jnp.cos(x) + 0.14128 * jnp.cos(2.0 * x) - 0.01168 * jnp.cos(3.0 * x)
    scale = (taper / jnp.float32(math.sqrt(CH)))[:, None]
    upper = jnp.concatenate([cosine * scale, -sine * scale], axis=1)
    lower = jnp.concatenate([sine * scale, cosine * scale], axis=1)
    return jnp.concatenate([upper, lower], axis=0).astype(jnp.bfloat16)


def _partner_pairs(n, fn):
    return [(i, fn(i)) for i in range(n)]


def _allreduce_sum(x, axis, n):
    if n & (n - 1):
        return lax.psum(x, axis)
    d = 1
    while d < n:
        x = x + lax.ppermute(x, axis, _partner_pairs(n, lambda i, d=d: i ^ d))
        d *= 2
    return x


def _gather_pair(part, matrix, pick2, parity, chip, n_owners, slots_dev):
    pairs = n_owners // 2
    contrib = jnp.einsum("bcr,brf->bcf", matrix, part, preferred_element_type=jnp.float32)
    high = contrib.astype(jnp.bfloat16)
    low = (contrib - high.astype(jnp.float32)).astype(jnp.bfloat16)
    partial = jnp.einsum(
        "sb,bcf->scf",
        pick2,
        jnp.concatenate([high, low], axis=0),
        preferred_element_type=jnp.float32,
    ).astype(jnp.bfloat16)
    partial = partial.reshape((2, pairs, slots_dev) + partial.shape[1:])

    mine = lax.dynamic_index_in_dim(partial, parity, axis=0, keepdims=False)
    other = lax.dynamic_index_in_dim(partial, 1 - parity, axis=0, keepdims=False)
    got = lax.ppermute(other, "uv", _partner_pairs(n_owners, lambda i: i ^ 1))
    pair_send = (mine.astype(jnp.float32) + got.astype(jnp.float32)).astype(jnp.bfloat16)
    own = lax.dynamic_index_in_dim(mine, chip, axis=0, keepdims=False).astype(
        jnp.float32
    ) + lax.dynamic_index_in_dim(got, chip, axis=0, keepdims=False).astype(jnp.float32)
    return pair_send, own


def _scatter_pairs(pair_send, own, chip, n_owners):
    pairs = n_owners // 2
    grid = own
    for d in range(1, pairs):
        if pairs & (pairs - 1):
            dest = lambda c, d=d: (c + d) % pairs
        else:
            dest = lambda c, d=d: c ^ d
        send = lax.dynamic_index_in_dim(pair_send, dest(chip), axis=0, keepdims=False)
        recv = lax.ppermute(
            send, "uv", _partner_pairs(n_owners, lambda i, dest=dest: dest(i // 2) * 2 + i % 2)
        )
        grid = grid + recv.astype(jnp.float32)
    return grid.astype(jnp.bfloat16)


def _chan_delay(gridded, table_half, n_chan):
    me = lax.axis_index("chan")
    cells_part = gridded.shape[1] // n_chan
    width = gridded.shape[2]
    out = None
    for d in range(n_chan):
        dest = (me + d) % n_chan
        send = lax.dynamic_slice_in_dim(gridded, dest * cells_part, cells_part, axis=1)
        if d == 0:
            recv = send
        else:
            recv = lax.ppermute(send, "chan", [(i, (i + d) % n_chan) for i in range(n_chan)])
        src = (me - d) % n_chan
        rows = lax.dynamic_slice_in_dim(table_half, src * width, width, axis=0)
        term = jnp.dot(recv.reshape(-1, width), rows, preferred_element_type=jnp.float32)
        out = term if out is None else out + term
    return out


def body(vis, row_cell, tap_weight, tap_offset, block_tile, tile_owner, galaxy):
    n_owners = lax.axis_size("uv")
    n_chan = lax.axis_size("chan")
    pairs = n_owners // 2
    me = lax.axis_index("uv")
    parity = me % 2
    chip = me // 2
    nblocks = block_tile.shape[0]
    slots_dev = galaxy.shape[0]
    chan_dev = vis.shape[2]

    rank_of_tile = tile_ranks(tile_owner, n_owners)
    owner = tile_owner[block_tile]
    rank = rank_of_tile[block_tile]
    slot = (owner % 2) * (pairs * slots_dev) + (owner // 2) * slots_dev + rank
    n_slots = n_owners * slots_dev
    pick = (jnp.arange(n_slots, dtype=jnp.int32)[:, None] == slot[None, :]).astype(jnp.bfloat16)
    pick2 = jnp.concatenate([pick, pick], axis=1)

    blocks = vis.reshape(nblocks, BR, 2, chan_dev)
    cells = row_cell.reshape(nblocks, BR)
    weights = jnp.transpose(tap_weight.reshape(KT, nblocks, BR), (1, 0, 2))
    matrix = kernel_matrix(cells, weights, tap_offset)
    table = delay_table()
    first = _gather_pair(blocks[:, :, 0, :], matrix, pick2, parity, chip, n_owners, slots_dev)
    second = _gather_pair(blocks[:, :, 1, :], matrix, pick2, parity, chip, n_owners, slots_dev)
    out = None
    for k, (pair_send, own) in enumerate((first, second)):
        gridded = _scatter_pairs(pair_send, own, chip, n_owners)
        if k == 0:
            table, gridded = lax.optimization_barrier((table, gridded))
        half = table[k * CH:(k + 1) * CH]
        if k == 0:
            piece = lax.all_to_all(gridded, "chan", split_axis=1, concat_axis=2, tiled=True)
            term = jnp.dot(
                piece.reshape(-1, CH), half, preferred_element_type=jnp.float32
            )
        else:
            term = _chan_delay(gridded, half, n_chan)
        out = term if out is None else out + term
    count, cells_part = slots_dev, TC // n_chan
    delay = out.reshape(count, cells_part, 2 * CH)
    galaxy_f = galaxy.astype(jnp.float32)
    product = delay[..., :CH] * galaxy_f[..., :CH] + delay[..., CH:] * galaxy_f[..., CH:]
    local_power = jnp.sum(product, axis=1)
    power = _allreduce_sum(local_power, "chan", n_chan) / jnp.float32(math.sqrt(TC))
    return (delay.astype(jnp.bfloat16), power)


def solution(mesh):
    return jax.shard_map(
        body,
        mesh=mesh,
        in_specs=(
            P("uv", None, "chan"),
            P("uv"),
            P(None, "uv"),
            P(),
            P("uv"),
            P(),
            P("uv", "chan", None),
        ),
        out_specs=(P("uv", "chan", None), P("uv", None)),
        check_vma=False,
    )
```

```python
import math

import jax
import jax.numpy as jnp
from jax import lax
from jax.sharding import PartitionSpec as P

CH = 1024
BR = 128
TC = 128
KT = 8


def tile_ranks(tile_owner, owners):
    onehot = (tile_owner[:, None] == jnp.arange(owners, dtype=jnp.int32)[None, :]).astype(jnp.int32)
    before = jnp.cumsum(onehot, axis=0) - onehot
    return jnp.sum(before * onehot, axis=1)


def kernel_matrix(cells, weights, tap_offset):
    positions = jnp.arange(TC, dtype=jnp.int32)
    total = jnp.zeros(cells.shape[:-1] + (TC, cells.shape[-1]), jnp.float32)
    for k in range(KT):
        target = cells + tap_offset[k]
        hit = target[..., None, :] == positions[:, None]
        total = total + jnp.where(
            hit, weights[..., k, :].astype(jnp.float32)[..., None, :], jnp.float32(0.0)
        )
    return total.astype(jnp.bfloat16)


def delay_table():
    freq = jnp.arange(CH, dtype=jnp.int32)
    phase = (freq[:, None] * freq[None, :] % CH).astype(jnp.float32) * jnp.float32(
        2.0 * math.pi / CH
    )
    cosine = jnp.cos(phase)
    sine = jnp.sin(phase)
    x = freq.astype(jnp.float32) * jnp.float32(2.0 * math.pi / CH)
    taper = 0.35875 - 0.48829 * jnp.cos(x) + 0.14128 * jnp.cos(2.0 * x) - 0.01168 * jnp.cos(3.0 * x)
    scale = (taper / jnp.float32(math.sqrt(CH)))[:, None]
    upper = jnp.concatenate([cosine * scale, -sine * scale], axis=1)
    lower = jnp.concatenate([sine * scale, cosine * scale], axis=1)
    return jnp.concatenate([upper, lower], axis=0).astype(jnp.bfloat16)


def _partner_pairs(n, fn):
    return [(i, fn(i)) for i in range(n)]


def _allreduce_sum(x, axis, n):
    if n & (n - 1):
        return lax.psum(x, axis)
    d = 1
    while d < n:
        x = x + lax.ppermute(x, axis, _partner_pairs(n, lambda i, d=d: i ^ d))
        d *= 2
    return x


def _gather_pair(part, matrix, pick2, parity, chip, n_owners, slots_dev):
    pairs = n_owners // 2
    contrib = jnp.einsum("bcr,brf->bcf", matrix, part, preferred_element_type=jnp.float32)
    high = contrib.astype(jnp.bfloat16)
    low = (contrib - high.astype(jnp.float32)).astype(jnp.bfloat16)
    partial = jnp.einsum(
        "sb,bcf->scf",
        pick2,
        jnp.concatenate([high, low], axis=0),
        preferred_element_type=jnp.float32,
    ).astype(jnp.bfloat16)
    partial = partial.reshape((2, pairs, slots_dev) + partial.shape[1:])

    mine = lax.dynamic_index_in_dim(partial, parity, axis=0, keepdims=False)
    other = lax.dynamic_index_in_dim(partial, 1 - parity, axis=0, keepdims=False)
    got = lax.ppermute(other, "uv", _partner_pairs(n_owners, lambda i: i ^ 1))
    pair_send = (mine.astype(jnp.float32) + got.astype(jnp.float32)).astype(jnp.bfloat16)
    own = lax.dynamic_index_in_dim(mine, chip, axis=0, keepdims=False).astype(
        jnp.float32
    ) + lax.dynamic_index_in_dim(got, chip, axis=0, keepdims=False).astype(jnp.float32)
    return pair_send, own


def _scatter_pairs(pair_send, own, chip, n_owners):
    pairs = n_owners // 2
    grid = own
    for d in range(1, pairs):
        if pairs & (pairs - 1):
            dest = lambda c, d=d: (c + d) % pairs
        else:
            dest = lambda c, d=d: c ^ d
        send = lax.dynamic_index_in_dim(pair_send, dest(chip), axis=0, keepdims=False)
        recv = lax.ppermute(
            send, "uv", _partner_pairs(n_owners, lambda i, dest=dest: dest(i // 2) * 2 + i % 2)
        )
        grid = grid + recv.astype(jnp.float32)
    gridded = grid.astype(jnp.bfloat16)
    return lax.all_to_all(gridded, "chan", split_axis=1, concat_axis=2, tiled=True)


def body(vis, row_cell, tap_weight, tap_offset, block_tile, tile_owner, galaxy):
    n_owners = lax.axis_size("uv")
    n_chan = lax.axis_size("chan")
    pairs = n_owners // 2
    me = lax.axis_index("uv")
    parity = me % 2
    chip = me // 2
    nblocks = block_tile.shape[0]
    slots_dev = galaxy.shape[0]
    chan_dev = vis.shape[2]

    rank_of_tile = tile_ranks(tile_owner, n_owners)
    owner = tile_owner[block_tile]
    rank = rank_of_tile[block_tile]
    slot = (owner % 2) * (pairs * slots_dev) + (owner // 2) * slots_dev + rank
    n_slots = n_owners * slots_dev
    pick = (jnp.arange(n_slots, dtype=jnp.int32)[:, None] == slot[None, :]).astype(jnp.bfloat16)
    pick2 = jnp.concatenate([pick, pick], axis=1)

    blocks = vis.reshape(nblocks, BR, 2, chan_dev)
    cells = row_cell.reshape(nblocks, BR)
    weights = jnp.transpose(tap_weight.reshape(KT, nblocks, BR), (1, 0, 2))
    matrix = kernel_matrix(cells, weights, tap_offset)
    matrix = lax.optimization_barrier(matrix)
    table = delay_table()
    first = _gather_pair(blocks[:, :, 0, :], matrix, pick2, parity, chip, n_owners, slots_dev)
    second = _gather_pair(blocks[:, :, 1, :], matrix, pick2, parity, chip, n_owners, slots_dev)
    table, second = lax.optimization_barrier((table, second))
    out = None
    for k, (pair_send, own) in enumerate((first, second)):
        piece = _scatter_pairs(pair_send, own, chip, n_owners)
        count, cells_part = piece.shape[0], piece.shape[1]
        term = jnp.dot(
            piece.reshape(count * cells_part, CH),
            table[k * CH:(k + 1) * CH],
            preferred_element_type=jnp.float32,
        )
        out = term if out is None else out + term
    delay = out.reshape(count, cells_part, 2 * CH)
    galaxy_f = galaxy.astype(jnp.float32)
    product = delay[..., :CH] * galaxy_f[..., :CH] + delay[..., CH:] * galaxy_f[..., CH:]
    local_power = jnp.sum(product, axis=1)
    power = _allreduce_sum(local_power, "chan", n_chan) / jnp.float32(math.sqrt(TC))
    return (delay.astype(jnp.bfloat16), power)


def solution(mesh):
    return jax.shard_map(
        body,
        mesh=mesh,
        in_specs=(
            P("uv", None, "chan"),
            P("uv"),
            P(None, "uv"),
            P(),
            P("uv"),
            P(),
            P("uv", "chan", None),
        ),
        out_specs=(P("uv", "chan", None), P("uv", None)),
        check_vma=False,
    )
```

```python
import math

import jax
import jax.numpy as jnp
from jax import lax
from jax.sharding import PartitionSpec as P

CH = 1024
BR = 128
TC = 128
KT = 8


def tile_ranks(tile_owner, owners):
    onehot = (tile_owner[:, None] == jnp.arange(owners, dtype=jnp.int32)[None, :]).astype(jnp.int32)
    before = jnp.cumsum(onehot, axis=0) - onehot
    return jnp.sum(before * onehot, axis=1)


def kernel_matrix(cells, weights, tap_offset):
    positions = jnp.arange(TC, dtype=jnp.int32)
    total = jnp.zeros(cells.shape[:-1] + (TC, cells.shape[-1]), jnp.float32)
    for k in range(KT):
        target = cells + tap_offset[k]
        hit = target[..., None, :] == positions[:, None]
        total = total + jnp.where(
            hit, weights[..., k, :].astype(jnp.float32)[..., None, :], jnp.float32(0.0)
        )
    return total.astype(jnp.bfloat16)


def delay_table():
    freq = jnp.arange(CH, dtype=jnp.int32)
    phase = (freq[:, None] * freq[None, :] % CH).astype(jnp.float32) * jnp.float32(
        2.0 * math.pi / CH
    )
    cosine = jnp.cos(phase)
    sine = jnp.sin(phase)
    x = freq.astype(jnp.float32) * jnp.float32(2.0 * math.pi / CH)
    taper = 0.35875 - 0.48829 * jnp.cos(x) + 0.14128 * jnp.cos(2.0 * x) - 0.01168 * jnp.cos(3.0 * x)
    scale = (taper / jnp.float32(math.sqrt(CH)))[:, None]
    upper = jnp.concatenate([cosine * scale, -sine * scale], axis=1)
    lower = jnp.concatenate([sine * scale, cosine * scale], axis=1)
    return jnp.concatenate([upper, lower], axis=0).astype(jnp.bfloat16)


def _partner_pairs(n, fn):
    return [(i, fn(i)) for i in range(n)]


def _allreduce_sum(x, axis, n):
    if n & (n - 1):
        return lax.psum(x, axis)
    d = 1
    while d < n:
        x = x + lax.ppermute(x, axis, _partner_pairs(n, lambda i, d=d: i ^ d))
        d *= 2
    return x


def _gather_pair(part, matrix, pick2, parity, chip, n_owners, slots_dev):
    pairs = n_owners // 2
    contrib = jnp.einsum("bcr,brf->bcf", matrix, part, preferred_element_type=jnp.float32)
    high = contrib.astype(jnp.bfloat16)
    low = (contrib - high.astype(jnp.float32)).astype(jnp.bfloat16)
    partial = jnp.einsum(
        "sb,bcf->scf",
        pick2,
        jnp.concatenate([high, low], axis=0),
        preferred_element_type=jnp.float32,
    ).astype(jnp.bfloat16)
    partial = partial.reshape((2, pairs, slots_dev) + partial.shape[1:])

    mine = lax.dynamic_index_in_dim(partial, parity, axis=0, keepdims=False)
    other = lax.dynamic_index_in_dim(partial, 1 - parity, axis=0, keepdims=False)
    got = lax.ppermute(other, "uv", _partner_pairs(n_owners, lambda i: i ^ 1))
    pair_send = (mine.astype(jnp.float32) + got.astype(jnp.float32)).astype(jnp.bfloat16)
    own = lax.dynamic_index_in_dim(mine, chip, axis=0, keepdims=False).astype(
        jnp.float32
    ) + lax.dynamic_index_in_dim(got, chip, axis=0, keepdims=False).astype(jnp.float32)
    return pair_send, own


def _scatter_pairs(pair_send, own, chip, n_owners):
    pairs = n_owners // 2
    grid = own
    for d in range(1, pairs):
        if pairs & (pairs - 1):
            dest = lambda c, d=d: (c + d) % pairs
        else:
            dest = lambda c, d=d: c ^ d
        send = lax.dynamic_index_in_dim(pair_send, dest(chip), axis=0, keepdims=False)
        recv = lax.ppermute(
            send, "uv", _partner_pairs(n_owners, lambda i, dest=dest: dest(i // 2) * 2 + i % 2)
        )
        grid = grid + recv.astype(jnp.float32)
    gridded = grid.astype(jnp.bfloat16)
    return lax.all_to_all(gridded, "chan", split_axis=1, concat_axis=2, tiled=True)


def body(vis, row_cell, tap_weight, tap_offset, block_tile, tile_owner, galaxy):
    n_owners = lax.axis_size("uv")
    n_chan = lax.axis_size("chan")
    pairs = n_owners // 2
    me = lax.axis_index("uv")
    parity = me % 2
    chip = me // 2
    nblocks = block_tile.shape[0]
    slots_dev = galaxy.shape[0]
    chan_dev = vis.shape[2]

    rank_of_tile = tile_ranks(tile_owner, n_owners)
    owner = tile_owner[block_tile]
    rank = rank_of_tile[block_tile]
    slot = (owner % 2) * (pairs * slots_dev) + (owner // 2) * slots_dev + rank
    n_slots = n_owners * slots_dev
    pick = (jnp.arange(n_slots, dtype=jnp.int32)[:, None] == slot[None, :]).astype(jnp.bfloat16)
    pick2 = jnp.concatenate([pick, pick], axis=1)

    blocks = vis.reshape(nblocks, BR, 2, chan_dev)
    cells = row_cell.reshape(nblocks, BR)
    weights = jnp.transpose(tap_weight.reshape(KT, nblocks, BR), (1, 0, 2))
    matrix = kernel_matrix(cells, weights, tap_offset)
    table = delay_table()
    first = _gather_pair(blocks[:, :, 0, :], matrix, pick2, parity, chip, n_owners, slots_dev)
    second = _gather_pair(blocks[:, :, 1, :], matrix, pick2, parity, chip, n_owners, slots_dev)
    table, second = lax.optimization_barrier((table, second))
    galaxy_f = galaxy.astype(jnp.float32)
    out = None
    for k, (pair_send, own) in enumerate((first, second)):
        piece = _scatter_pairs(pair_send, own, chip, n_owners)
        count, cells_part = piece.shape[0], piece.shape[1]
        term = jnp.dot(
            piece.reshape(count * cells_part, CH),
            table[k * CH:(k + 1) * CH],
            preferred_element_type=jnp.float32,
        )
        part = term.reshape(count, cells_part, 2 * CH)
        power_part = jnp.sum(
            part[..., :CH] * galaxy_f[..., :CH] + part[..., CH:] * galaxy_f[..., CH:], axis=1
        )
        out = part if out is None else out + part
        local_power = power_part if k == 0 else local_power + power_part
    delay = out
    power = _allreduce_sum(local_power, "chan", n_chan) / jnp.float32(math.sqrt(TC))
    return (delay.astype(jnp.bfloat16), power)


def solution(mesh):
    return jax.shard_map(
        body,
        mesh=mesh,
        in_specs=(
            P("uv", None, "chan"),
            P("uv"),
            P(None, "uv"),
            P(),
            P("uv"),
            P(),
            P("uv", "chan", None),
        ),
        out_specs=(P("uv", "chan", None), P("uv", None)),
        check_vma=False,
    )
```

```python
import math

import jax
import jax.numpy as jnp
from jax import lax
from jax.sharding import PartitionSpec as P

CH = 1024
BR = 128
TC = 128
KT = 8


def tile_ranks(tile_owner, owners):
    onehot = (tile_owner[:, None] == jnp.arange(owners, dtype=jnp.int32)[None, :]).astype(jnp.int32)
    before = jnp.cumsum(onehot, axis=0) - onehot
    return jnp.sum(before * onehot, axis=1)


def kernel_matrix(cells, weights, tap_offset):
    positions = jnp.arange(TC, dtype=jnp.int32)
    total = jnp.zeros(cells.shape[:-1] + (TC, cells.shape[-1]), jnp.float32)
    for k in range(KT):
        target = cells + tap_offset[k]
        hit = target[..., None, :] == positions[:, None]
        total = total + jnp.where(
            hit, weights[..., k, :].astype(jnp.float32)[..., None, :], jnp.float32(0.0)
        )
    return total.astype(jnp.bfloat16)


def delay_table():
    freq = jnp.arange(CH, dtype=jnp.int32)
    phase = (freq[:, None] * freq[None, :] % CH).astype(jnp.float32) * jnp.float32(
        2.0 * math.pi / CH
    )
    cosine = jnp.cos(phase)
    sine = jnp.sin(phase)
    x = freq.astype(jnp.float32) * jnp.float32(2.0 * math.pi / CH)
    taper = 0.35875 - 0.48829 * jnp.cos(x) + 0.14128 * jnp.cos(2.0 * x) - 0.01168 * jnp.cos(3.0 * x)
    scale = (taper / jnp.float32(math.sqrt(CH)))[:, None]
    upper = jnp.concatenate([cosine * scale, -sine * scale], axis=1)
    lower = jnp.concatenate([sine * scale, cosine * scale], axis=1)
    return jnp.concatenate([upper, lower], axis=0).astype(jnp.bfloat16)


def _partner_pairs(n, fn):
    return [(i, fn(i)) for i in range(n)]


def _allreduce_sum(x, axis, n):
    if n & (n - 1):
        return lax.psum(x, axis)
    d = 1
    while d < n:
        x = x + lax.ppermute(x, axis, _partner_pairs(n, lambda i, d=d: i ^ d))
        d *= 2
    return x


def _gather_pair(part, matrix, pick2, parity, chip, n_owners, slots_dev):
    pairs = n_owners // 2
    contrib = jnp.einsum("bcr,brf->bcf", matrix, part, preferred_element_type=jnp.float32)
    high = contrib.astype(jnp.bfloat16)
    low = (contrib - high.astype(jnp.float32)).astype(jnp.bfloat16)
    partial = jnp.einsum(
        "sb,bcf->scf",
        pick2,
        jnp.concatenate([high, low], axis=0),
        preferred_element_type=jnp.float32,
    ).astype(jnp.bfloat16)
    partial = partial.reshape((2, pairs, slots_dev) + partial.shape[1:])

    mine = lax.dynamic_index_in_dim(partial, parity, axis=0, keepdims=False)
    other = lax.dynamic_index_in_dim(partial, 1 - parity, axis=0, keepdims=False)
    got = lax.ppermute(other, "uv", _partner_pairs(n_owners, lambda i: i ^ 1))
    pair_send = (mine.astype(jnp.float32) + got.astype(jnp.float32)).astype(jnp.bfloat16)
    own = lax.dynamic_index_in_dim(mine, chip, axis=0, keepdims=False).astype(
        jnp.float32
    ) + lax.dynamic_index_in_dim(got, chip, axis=0, keepdims=False).astype(jnp.float32)
    return pair_send, own


def _scatter_pairs(pair_send, own, chip, n_owners):
    pairs = n_owners // 2
    grid = own
    for d in range(1, pairs):
        if pairs & (pairs - 1):
            dest = lambda c, d=d: (c + d) % pairs
        else:
            dest = lambda c, d=d: c ^ d
        send = lax.dynamic_index_in_dim(pair_send, dest(chip), axis=0, keepdims=False)
        recv = lax.ppermute(
            send, "uv", _partner_pairs(n_owners, lambda i, dest=dest: dest(i // 2) * 2 + i % 2)
        )
        grid = grid + recv.astype(jnp.float32)
    gridded = grid.astype(jnp.bfloat16)
    return lax.all_to_all(gridded, "chan", split_axis=1, concat_axis=2, tiled=True)


def body(vis, row_cell, tap_weight, tap_offset, block_tile, tile_owner, galaxy):
    n_owners = lax.axis_size("uv")
    n_chan = lax.axis_size("chan")
    pairs = n_owners // 2
    me = lax.axis_index("uv")
    parity = me % 2
    chip = me // 2
    nblocks = block_tile.shape[0]
    slots_dev = galaxy.shape[0]
    chan_dev = vis.shape[2]

    rank_of_tile = tile_ranks(tile_owner, n_owners)
    owner = tile_owner[block_tile]
    rank = rank_of_tile[block_tile]
    slot = (owner % 2) * (pairs * slots_dev) + (owner // 2) * slots_dev + rank
    n_slots = n_owners * slots_dev
    pick = (jnp.arange(n_slots, dtype=jnp.int32)[:, None] == slot[None, :]).astype(jnp.bfloat16)
    pick2 = jnp.concatenate([pick, pick], axis=1)

    blocks = vis.reshape(nblocks, BR, 2, chan_dev)
    cells = row_cell.reshape(nblocks, BR)
    weights = jnp.transpose(tap_weight.reshape(KT, nblocks, BR), (1, 0, 2))
    matrix = kernel_matrix(cells, weights, tap_offset)
    table = delay_table()
    first = _gather_pair(blocks[:, :, 0, :], matrix, pick2, parity, chip, n_owners, slots_dev)
    second = _gather_pair(blocks[:, :, 1, :], matrix, pick2, parity, chip, n_owners, slots_dev)
    table, second = lax.optimization_barrier((table, second))
    out = None
    for k, (pair_send, own) in ((1, second), (0, first)):
        piece = _scatter_pairs(pair_send, own, chip, n_owners)
        count, cells_part = piece.shape[0], piece.shape[1]
        term = jnp.dot(
            piece.reshape(count * cells_part, CH),
            table[k * CH:(k + 1) * CH],
            preferred_element_type=jnp.float32,
        )
        out = term if out is None else out + term
    delay = out.reshape(count, cells_part, 2 * CH)
    galaxy_f = galaxy.astype(jnp.float32)
    product = delay[..., :CH] * galaxy_f[..., :CH] + delay[..., CH:] * galaxy_f[..., CH:]
    local_power = jnp.sum(product, axis=1)
    power = _allreduce_sum(local_power, "chan", n_chan) / jnp.float32(math.sqrt(TC))
    return (delay.astype(jnp.bfloat16), power)


def solution(mesh):
    return jax.shard_map(
        body,
        mesh=mesh,
        in_specs=(
            P("uv", None, "chan"),
            P("uv"),
            P(None, "uv"),
            P(),
            P("uv"),
            P(),
            P("uv", "chan", None),
        ),
        out_specs=(P("uv", "chan", None), P("uv", None)),
        check_vma=False,
    )
```

```python
import math

import jax
import jax.numpy as jnp
from jax import lax
from jax.sharding import PartitionSpec as P

CH = 1024
BR = 128
TC = 128
KT = 8


def tile_ranks(tile_owner, owners):
    onehot = (tile_owner[:, None] == jnp.arange(owners, dtype=jnp.int32)[None, :]).astype(jnp.int32)
    before = jnp.cumsum(onehot, axis=0) - onehot
    return jnp.sum(before * onehot, axis=1)


def kernel_matrix(cells, weights, tap_offset):
    positions = jnp.arange(TC, dtype=jnp.int32)
    total = jnp.zeros(cells.shape[:-1] + (TC, cells.shape[-1]), jnp.float32)
    for k in range(KT):
        target = cells + tap_offset[k]
        hit = target[..., None, :] == positions[:, None]
        total = total + jnp.where(
            hit, weights[..., k, :].astype(jnp.float32)[..., None, :], jnp.float32(0.0)
        )
    return total.astype(jnp.bfloat16)


def delay_table():
    freq = jnp.arange(CH, dtype=jnp.int32)
    phase = (freq[:, None] * freq[None, :] % CH).astype(jnp.float32) * jnp.float32(
        2.0 * math.pi / CH
    )
    cosine = jnp.cos(phase)
    sine = jnp.sin(phase)
    x = freq.astype(jnp.float32) * jnp.float32(2.0 * math.pi / CH)
    taper = 0.35875 - 0.48829 * jnp.cos(x) + 0.14128 * jnp.cos(2.0 * x) - 0.01168 * jnp.cos(3.0 * x)
    scale = (taper / jnp.float32(math.sqrt(CH)))[:, None]
    upper = jnp.concatenate([cosine * scale, -sine * scale], axis=1)
    lower = jnp.concatenate([sine * scale, cosine * scale], axis=1)
    return jnp.concatenate([upper, lower], axis=0).astype(jnp.bfloat16)


def _partner_pairs(n, fn):
    return [(i, fn(i)) for i in range(n)]


def _allreduce_sum(x, axis, n):
    if n & (n - 1):
        return lax.psum(x, axis)
    d = 1
    while d < n:
        x = x + lax.ppermute(x, axis, _partner_pairs(n, lambda i, d=d: i ^ d))
        d *= 2
    return x


def _gather_pair(part, matrix, pick2, parity, chip, n_owners, slots_dev):
    pairs = n_owners // 2
    contrib = jnp.einsum("bcr,brf->bcf", matrix, part, preferred_element_type=jnp.float32)
    high = contrib.astype(jnp.bfloat16)
    low = (contrib - high.astype(jnp.float32)).astype(jnp.bfloat16)
    partial = jnp.einsum(
        "sb,bcf->scf",
        pick2,
        jnp.concatenate([high, low], axis=0),
        preferred_element_type=jnp.float32,
    ).astype(jnp.bfloat16)
    partial = partial.reshape((2, pairs, slots_dev) + partial.shape[1:])

    mine = lax.dynamic_index_in_dim(partial, parity, axis=0, keepdims=False)
    other = lax.dynamic_index_in_dim(partial, 1 - parity, axis=0, keepdims=False)
    got = lax.ppermute(other, "uv", _partner_pairs(n_owners, lambda i: i ^ 1))
    pair_send = (mine.astype(jnp.float32) + got.astype(jnp.float32)).astype(jnp.bfloat16)
    own = lax.dynamic_index_in_dim(mine, chip, axis=0, keepdims=False).astype(
        jnp.float32
    ) + lax.dynamic_index_in_dim(got, chip, axis=0, keepdims=False).astype(jnp.float32)
    return pair_send, own


def _scatter_pairs(pair_send, own, chip, n_owners):
    pairs = n_owners // 2
    grid = own
    for d in range(1, pairs):
        if pairs & (pairs - 1):
            dest = lambda c, d=d: (c + d) % pairs
        else:
            dest = lambda c, d=d: c ^ d
        send = lax.dynamic_index_in_dim(pair_send, dest(chip), axis=0, keepdims=False)
        recv = lax.ppermute(
            send, "uv", _partner_pairs(n_owners, lambda i, dest=dest: dest(i // 2) * 2 + i % 2)
        )
        grid = grid + recv.astype(jnp.float32)
    gridded = grid.astype(jnp.bfloat16)
    return lax.all_to_all(gridded, "chan", split_axis=1, concat_axis=2, tiled=True)


def body(vis, row_cell, tap_weight, tap_offset, block_tile, tile_owner, galaxy):
    n_owners = lax.axis_size("uv")
    n_chan = lax.axis_size("chan")
    pairs = n_owners // 2
    me = lax.axis_index("uv")
    parity = me % 2
    chip = me // 2
    nblocks = block_tile.shape[0]
    slots_dev = galaxy.shape[0]
    chan_dev = vis.shape[2]

    rank_of_tile = tile_ranks(tile_owner, n_owners)
    owner = tile_owner[block_tile]
    rank = rank_of_tile[block_tile]
    slot = (owner % 2) * (pairs * slots_dev) + (owner // 2) * slots_dev + rank
    n_slots = n_owners * slots_dev
    pick = (jnp.arange(n_slots, dtype=jnp.int32)[:, None] == slot[None, :]).astype(jnp.bfloat16)
    pick2 = jnp.concatenate([pick, pick], axis=1)

    blocks = vis.reshape(nblocks, BR, 2, chan_dev)
    cells = row_cell.reshape(nblocks, BR)
    weights = jnp.transpose(tap_weight.reshape(KT, nblocks, BR), (1, 0, 2))
    matrix = kernel_matrix(cells, weights, tap_offset)
    table = delay_table()
    first = _gather_pair(blocks[:, :, 0, :], matrix, pick2, parity, chip, n_owners, slots_dev)
    second = _gather_pair(blocks[:, :, 1, :], matrix, pick2, parity, chip, n_owners, slots_dev)
    table, second = lax.optimization_barrier((table, second))
    galaxy = lax.optimization_barrier((galaxy, first[1]))[0]
    out = None
    for k, (pair_send, own) in enumerate((first, second)):
        piece = _scatter_pairs(pair_send, own, chip, n_owners)
        count, cells_part = piece.shape[0], piece.shape[1]
        term = jnp.dot(
            piece.reshape(count * cells_part, CH),
            table[k * CH:(k + 1) * CH],
            preferred_element_type=jnp.float32,
        )
        out = term if out is None else out + term
    delay = out.reshape(count, cells_part, 2 * CH)
    galaxy_f = galaxy.astype(jnp.float32)
    product = delay[..., :CH] * galaxy_f[..., :CH] + delay[..., CH:] * galaxy_f[..., CH:]
    local_power = jnp.sum(product, axis=1)
    power = _allreduce_sum(local_power, "chan", n_chan) / jnp.float32(math.sqrt(TC))
    return (delay.astype(jnp.bfloat16), power)


def solution(mesh):
    return jax.shard_map(
        body,
        mesh=mesh,
        in_specs=(
            P("uv", None, "chan"),
            P("uv"),
            P(None, "uv"),
            P(),
            P("uv"),
            P(),
            P("uv", "chan", None),
        ),
        out_specs=(P("uv", "chan", None), P("uv", None)),
        check_vma=False,
    )
```
